128 devices in a mesh: comp: 4 (over z), band: 32 (over y, x, core).
Axes of the slice: x: 4, y: 4, z: 4, core: 2. Of those that a mesh axis runs over, the one named last changes fastest.
Arguments:
- layer_temp: float32 [4, 2048, 16, 256], P('comp', 'band'), may hold values from -6 to 6
- diffusivity: float32 [4, 2048, 256], P('comp', 'band'), may hold values from 0.02 to 0.11
- owner_band: int32 [4, 2048, 1], P('comp', 'band'), may hold values from 0 to 31, as said below
- block_index: int32 [4, 2048], P('comp', 'band'), may hold values from 0 to 63
- remap_blocks: bfloat16 [4, 2048, 256, 256], P('comp', 'band'), may hold values from -0.375 to 0.375
Outputs:
- temp_out: float32 [4, 2048, 16, 256], P('comp', 'band')
- surface_temp: bfloat16 [4, 2048, 4, 256], P('comp', 'band')
The draws below stay inside these ranges and needn't reach their ends.
Inputs may be any that keep to these rules, and one draw needn't show every extreme that they name: `owner_band`: among the rows of one device no band is named by more than 4 rows, and some band is named by exactly 4.
All inputs are finite; a program needn't handle non-finite values.
Results may differ from the reference program's by a relative error of at most 0.0055.
Values may be sent and summed in bfloat16 or wider, within the bound.
No kernel may reach another device: no remote copies, remote signals or barrier semaphores. Data moves between devices by JAX's collectives and lax.ppermute only.
A program may use at most 64 MiB of HBM per device.

```python
import math
import jax
import jax.numpy as jnp
from jax import lax

ROWS = 64
COLS = 256
LEV = 16
NF = 4
NSTEPS = 4
NR = 2048
CAP = 4
N_COMP = 4
N_BAND = 32


def draw_owner_band(key, part):
    group_count = -(-ROWS // CAP)
    block_keys = jax.random.split(jax.random.fold_in(key, 11), N_COMP * N_BAND)
    orders = jax.vmap(lambda single: jax.random.permutation(single, ROWS))(block_keys)
    orders = orders.astype(jnp.int32).reshape(N_COMP, N_BAND, ROWS)
    offsets = jax.random.randint(jax.random.fold_in(key, 12), (N_COMP, N_BAND), 0, max(1, group_count - 2)).astype(jnp.int32)
    own_band = jnp.arange(N_BAND, dtype=jnp.int32)[None, :]
    starting = own_band - 1 - offsets
    owners = (starting[:, :, None] + orders // CAP) % N_BAND
    return owners.astype(jnp.int32).reshape(N_COMP, NR, 1)


def place_ends(array, own_key, smallest, largest):
    longest = array.shape.index(max(array.shape))
    spots = []
    for shift in (0, 1):
        where = [jax.random.randint(jax.random.fold_in(own_key, axis), (), 0, length) for axis, length in enumerate(array.shape)]
        where[longest] = (where[longest] + shift) % array.shape[longest]
        spots.append(tuple(where))
    return array.at[spots[0]].set(smallest).at[spots[1]].set(largest)


def steps_of(rng, extent, cuts, smallest, top_value):
    def one(axis_at, shards_of):
        heights = jax.random.uniform(jax.random.fold_in(jax.random.fold_in(rng, 6), axis_at), (shards_of,), jnp.float32, smallest / len(cuts), top_value / len(cuts))
        return jnp.repeat(jnp.exp(heights), extent[axis_at] // shards_of).reshape((-1,) + (1,) * (len(extent) - axis_at - 1))

    factor_of = one(*cuts[0])
    for cut in cuts[1:]:
        factor_of = factor_of * one(*cut)
    return factor_of


def centred(own_key, dims, width, limit, pieces=(), kind=jnp.bfloat16):
    drawn = width * jax.random.normal(own_key, dims, jnp.float32)
    if pieces:
        drawn = drawn * steps_of(own_key, dims, pieces, -0.22, 0.18)
    return jnp.clip(drawn, -limit, limit).astype(kind)


def setup_inputs(seed: int = 0) -> dict:
    keys = jax.random.split(jax.random.key(seed), 6)
    return {
        "layer_temp": centred(keys[0], (N_COMP, NR, LEV, COLS), 1.0, 6.0, ((0, 4), (1, 32)), jnp.float32),
        "diffusivity": jnp.clip(jnp.exp(math.log(0.11) - 1.7047481 * jax.random.uniform(keys[1], (N_COMP, NR, COLS), jnp.float32) ** steps_of(keys[1], (N_COMP, NR, COLS), ((0, 4), (1, 32)), -0.2, 0.2)), 0.02, 0.11),
        "owner_band": draw_owner_band(jax.random.fold_in(keys[5], 71), 0),
        "block_index": place_ends(jax.random.randint(keys[3], (N_COMP, NR), 0, ROWS), jax.random.fold_in(keys[3], 1), 0, ROWS - 1).astype(jnp.int32),
        "remap_blocks": centred(keys[4], (N_COMP, NR, COLS, COLS), COLS ** -0.5, 0.375, ((0, 4), (1, 32))),
    }


COUPLING = 0.25
VERTICAL = 0.15


def advance(fields, diffusivity):
    padded = jnp.pad(fields, ((0, 0), (1, 1), (0, 0), (0, 0)))
    row_north = padded[:, :-2]
    row_south = padded[:, 2:]
    col_east = jnp.roll(fields, 1, axis=3)
    col_west = jnp.roll(fields, -1, axis=3)
    level_below = jnp.concatenate([fields[:, :, :1], fields[:, :, :-1]], axis=2)
    level_above = jnp.concatenate([fields[:, :, 1:], fields[:, :, -1:]], axis=2)
    horizontal = row_north + row_south + col_east + col_west - 4.0 * fields
    return fields + diffusivity[:, :, None, :] * horizontal + VERTICAL * (level_below + level_above - 2.0 * fields)


def reference(layer_temp, diffusivity, owner_band, block_index, remap_blocks):
    stepped = layer_temp
    for step_index in range(NSTEPS):
        stepped = advance(stepped, diffusivity)
    surface_layers = lax.optimization_barrier(layer_temp[:, :, :NF, :].astype(jnp.bfloat16)).astype(jnp.float32)
    fluxes = []
    for section in range(N_COMP - 1):
        fluxes.append(jnp.einsum("rfc,rcd->rfd", surface_layers[section], remap_blocks[section].astype(jnp.float32)))
    flux_all = jnp.stack(fluxes)
    target = (owner_band[:N_COMP - 1, :, 0] * ROWS + block_index[:N_COMP - 1]).astype(jnp.int32)
    ocean_heat = jax.ops.segment_sum(flux_all.reshape(-1, NF, COLS), target.reshape(-1), num_segments=NR)
    ocean = stepped[N_COMP - 1]
    ocean = ocean.at[:, :NF].add(COUPLING * ocean_heat)
    temp_out = stepped.at[N_COMP - 1].set(ocean)
    sea_surface = lax.optimization_barrier(ocean[:, :NF].astype(jnp.bfloat16)).astype(jnp.float32)
    returned = jnp.einsum("rfc,rcd->rfd", sea_surface, remap_blocks[N_COMP - 1].astype(jnp.float32)).astype(jnp.bfloat16)
    atmosphere_side = returned[target]
    surface_temp = jnp.concatenate([atmosphere_side, returned[None]], axis=0)
    return temp_out, surface_temp
```

```python
import jax
import jax.numpy as jnp
from jax import lax
from jax.sharding import PartitionSpec as P

NF = 4
NSTEPS = 4
CAP = 4

COUPLING = 0.25
VERTICAL = 0.15
HIGHEST = lax.Precision.HIGHEST


def diffuse(layer_temp, diffusivity):
    n_bands = lax.axis_size("band")
    band = lax.axis_index("band")
    rows = layer_temp.shape[1]
    lev = layer_temp.shape[2]
    halo = NSTEPS
    comb = jnp.concatenate([layer_temp[0], diffusivity[0][:, None, :]], axis=1)
    forward = [(i, i + 1) for i in range(n_bands - 1)]
    backward = [(i + 1, i) for i in range(n_bands - 1)]
    above = lax.ppermute(comb[rows - halo:], "band", forward)
    below = lax.ppermute(comb[:halo], "band", backward)
    padded = jnp.concatenate([above, comb, below], axis=0)
    fields = padded[:, :lev]
    diff = padded[:, lev]
    grow = band * rows - halo + jnp.arange(rows + 2 * halo, dtype=jnp.int32)
    valid = ((grow >= 0) & (grow < n_bands * rows))[:, None, None]
    for _ in range(NSTEPS):
        row_north = jnp.roll(fields, 1, axis=0)
        row_south = jnp.roll(fields, -1, axis=0)
        col_east = jnp.roll(fields, 1, axis=2)
        col_west = jnp.roll(fields, -1, axis=2)
        level_below = jnp.concatenate([fields[:, :1], fields[:, :-1]], axis=1)
        level_above = jnp.concatenate([fields[:, 1:], fields[:, -1:]], axis=1)
        horizontal = row_north + row_south + col_east + col_west - 4.0 * fields
        fields = (
            fields
            + diff[:, None, :] * horizontal
            + VERTICAL * (level_below + level_above - 2.0 * fields)
        )
        fields = jnp.where(valid, fields, 0.0)
    return fields[halo:halo + rows]


def body(layer_temp, diffusivity, owner_band, block_index, remap_blocks):
    n_sections = lax.axis_size("comp")
    n_bands = lax.axis_size("band")
    section = lax.axis_index("comp")
    rows = layer_temp.shape[1]
    cols = layer_temp.shape[3]
    width = NF * cols
    is_ocean = section == n_sections - 1
    weights_local = remap_blocks[0]

    surface_layers = layer_temp[0, :, :NF, :].astype(jnp.bfloat16)
    flux = lax.cond(
        is_ocean,
        lambda: jnp.zeros((rows, NF, cols), jnp.float32),
        lambda: jnp.einsum(
            "rfc,rcd->rfd", surface_layers, weights_local, preferred_element_type=jnp.float32
        ),
    )

    destination = owner_band[0, :, 0]
    dest_onehot = (destination[:, None] == jnp.arange(n_bands, dtype=jnp.int32)[None, :]).astype(
        jnp.float32
    )
    positions = jnp.arange(rows, dtype=jnp.int32)
    earlier_mask = (positions[:, None] > positions[None, :]).astype(jnp.float32)
    earlier = jnp.dot(earlier_mask, dest_onehot, precision=HIGHEST)
    slot_rank = jnp.sum(earlier * dest_onehot, axis=1).astype(jnp.int32)
    slot_onehot = (slot_rank[:, None] == jnp.arange(CAP, dtype=jnp.int32)[None, :]).astype(
        jnp.float32
    )
    selector = (dest_onehot[:, :, None] * slot_onehot[:, None, :]).reshape(rows, n_bands * CAP)

    index_lanes = jnp.broadcast_to(block_index[0].astype(jnp.float32)[:, None], (rows, 128))
    payload = jnp.concatenate([flux.reshape(rows, width), index_lanes], axis=1)
    sending = jnp.einsum("rk,rx->kx", selector, payload, precision=HIGHEST)
    sending = sending.reshape(n_bands, CAP, width + 128)
    received = lax.all_to_all(sending, "band", 0, 0, tiled=True)
    received = received.reshape(n_bands * CAP, width + 128)
    got_index = received[:, width].astype(jnp.int32)
    match = (got_index[:, None] == positions[None, :]).astype(jnp.float32)
    partial = jnp.einsum("kr,kx->rx", match, received[:, :width], precision=HIGHEST)
    ocean_heat = lax.psum(partial, "comp")

    fields = diffuse(layer_temp, diffusivity)
    heating = jnp.where(is_ocean, COUPLING * ocean_heat, 0.0).reshape(rows, NF, cols)
    temp_out = fields.at[:, :NF].add(heating)
    sea_surface = temp_out[:, :NF].astype(jnp.bfloat16)
    returned = lax.cond(
        is_ocean,
        lambda: jnp.einsum(
            "rfc,rcd->rfd", sea_surface, weights_local, preferred_element_type=jnp.float32
        ).astype(jnp.bfloat16),
        lambda: jnp.zeros((rows, NF, cols), jnp.bfloat16),
    )

    gathered = lax.all_gather(returned, "comp", axis=0, tiled=False)
    ocean_rows = gathered[n_sections - 1].reshape(rows, width)
    reply = jnp.einsum(
        "kr,rx->kx", match.astype(jnp.bfloat16), ocean_rows, preferred_element_type=jnp.float32
    ).astype(jnp.bfloat16)
    reply = reply.reshape(n_bands, CAP, width)
    came_back = lax.all_to_all(reply, "band", 0, 0, tiled=True)
    came_back = came_back.reshape(n_bands * CAP, width)
    seen = jnp.einsum(
        "rk,kx->rx", selector.astype(jnp.bfloat16), came_back, preferred_element_type=jnp.float32
    ).astype(jnp.bfloat16)
    surface_temp = jnp.where(is_ocean, returned, seen.reshape(rows, NF, cols))
    return temp_out[None], surface_temp[None]


def solution(mesh):
    return jax.shard_map(
        body,
        mesh=mesh,
        in_specs=(
            P("comp", "band", None, None),
            P("comp", "band", None),
            P("comp", "band", None),
            P("comp", "band"),
            P("comp", "band", None, None),
        ),
        out_specs=(P("comp", "band", None, None), P("comp", "band", None, None)),
        check_vma=False,
    )
```

```python
import jax
import jax.numpy as jnp
from jax import lax
from jax.sharding import PartitionSpec as P

NF = 4
NSTEPS = 4
CAP = 4

COUPLING = 0.25
VERTICAL = 0.15
HIGHEST = lax.Precision.HIGHEST


def diffuse(layer_temp, diffusivity):
    n_bands = lax.axis_size("band")
    band = lax.axis_index("band")
    rows = layer_temp.shape[1]
    lev = layer_temp.shape[2]
    halo = NSTEPS
    comb = jnp.concatenate([layer_temp[0], diffusivity[0][:, None, :]], axis=1)
    forward = [(i, i + 1) for i in range(n_bands - 1)]
    backward = [(i + 1, i) for i in range(n_bands - 1)]
    above = lax.ppermute(comb[rows - halo:], "band", forward)
    below = lax.ppermute(comb[:halo], "band", backward)
    padded = jnp.concatenate([above, comb, below], axis=0)
    fields = padded[:, :lev]
    diff = padded[:, lev]
    grow = band * rows - halo + jnp.arange(rows + 2 * halo, dtype=jnp.int32)
    valid = ((grow >= 0) & (grow < n_bands * rows))[:, None, None]
    for _ in range(NSTEPS):
        row_north = jnp.roll(fields, 1, axis=0)
        row_south = jnp.roll(fields, -1, axis=0)
        col_east = jnp.roll(fields, 1, axis=2)
        col_west = jnp.roll(fields, -1, axis=2)
        level_below = jnp.concatenate([fields[:, :1], fields[:, :-1]], axis=1)
        level_above = jnp.concatenate([fields[:, 1:], fields[:, -1:]], axis=1)
        horizontal = row_north + row_south + col_east + col_west - 4.0 * fields
        fields = (
            fields
            + diff[:, None, :] * horizontal
            + VERTICAL * (level_below + level_above - 2.0 * fields)
        )
        fields = jnp.where(valid, fields, 0.0)
    return fields[halo:halo + rows]


def body(layer_temp, diffusivity, owner_band, block_index, remap_blocks):
    n_sections = lax.axis_size("comp")
    n_bands = lax.axis_size("band")
    section = lax.axis_index("comp")
    rows = layer_temp.shape[1]
    cols = layer_temp.shape[3]
    width = NF * cols
    is_ocean = section == n_sections - 1
    weights_local = remap_blocks[0]

    surface_layers = layer_temp[0, :, :NF, :].astype(jnp.bfloat16)
    flux = lax.cond(
        is_ocean,
        lambda: jnp.zeros((rows, NF, cols), jnp.float32),
        lambda: jnp.einsum(
            "rfc,rcd->rfd", surface_layers, weights_local, preferred_element_type=jnp.float32
        ),
    )

    destination = owner_band[0, :, 0]
    dest_onehot = (destination[:, None] == jnp.arange(n_bands, dtype=jnp.int32)[None, :]).astype(
        jnp.float32
    )
    positions = jnp.arange(rows, dtype=jnp.int32)
    earlier_mask = (positions[:, None] > positions[None, :]).astype(jnp.float32)
    earlier = jnp.dot(earlier_mask, dest_onehot, precision=HIGHEST)
    slot_rank = jnp.sum(earlier * dest_onehot, axis=1).astype(jnp.int32)
    slot_onehot = (slot_rank[:, None] == jnp.arange(CAP, dtype=jnp.int32)[None, :]).astype(
        jnp.float32
    )
    selector = (dest_onehot[:, :, None] * slot_onehot[:, None, :]).reshape(rows, n_bands * CAP)

    index_lanes = jnp.broadcast_to(block_index[0].astype(jnp.float32)[:, None], (rows, 128))
    payload = jnp.concatenate([flux.reshape(rows, width), index_lanes], axis=1)
    sending = jnp.einsum("rk,rx->kx", selector, payload, precision=HIGHEST)
    sending = sending.reshape(n_bands, CAP, width + 128)
    received = lax.all_to_all(sending, "band", 0, 0, tiled=True)
    received = received.reshape(n_bands * CAP, width + 128)
    got_index = received[:, width].astype(jnp.int32)
    match = (got_index[:, None] == positions[None, :]).astype(jnp.float32)
    partial = jnp.einsum("kr,kx->rx", match, received[:, :width], precision=HIGHEST)
    last = n_sections - 1
    ocean_heat = partial
    for source in range(last):
        ocean_heat = ocean_heat + lax.ppermute(partial, "comp", [(source, last)])

    fields = diffuse(layer_temp, diffusivity)
    heating = jnp.where(is_ocean, COUPLING * ocean_heat, 0.0).reshape(rows, NF, cols)
    temp_out = fields.at[:, :NF].add(heating)
    sea_surface = temp_out[:, :NF].astype(jnp.bfloat16)
    returned = lax.cond(
        is_ocean,
        lambda: jnp.einsum(
            "rfc,rcd->rfd", sea_surface, weights_local, preferred_element_type=jnp.float32
        ).astype(jnp.bfloat16),
        lambda: jnp.zeros((rows, NF, cols), jnp.bfloat16),
    )

    ocean_rows = returned
    for target in range(last):
        ocean_rows = ocean_rows + lax.ppermute(returned, "comp", [(last, target)])
    ocean_rows = ocean_rows.reshape(rows, width)
    reply = jnp.einsum(
        "kr,rx->kx", match.astype(jnp.bfloat16), ocean_rows, preferred_element_type=jnp.float32
    ).astype(jnp.bfloat16)
    reply = reply.reshape(n_bands, CAP, width)
    came_back = lax.all_to_all(reply, "band", 0, 0, tiled=True)
    came_back = came_back.reshape(n_bands * CAP, width)
    seen = jnp.einsum(
        "rk,kx->rx", selector.astype(jnp.bfloat16), came_back, preferred_element_type=jnp.float32
    ).astype(jnp.bfloat16)
    surface_temp = jnp.where(is_ocean, returned, seen.reshape(rows, NF, cols))
    return temp_out[None], surface_temp[None]


def solution(mesh):
    return jax.shard_map(
        body,
        mesh=mesh,
        in_specs=(
            P("comp", "band", None, None),
            P("comp", "band", None),
            P("comp", "band", None),
            P("comp", "band"),
            P("comp", "band", None, None),
        ),
        out_specs=(P("comp", "band", None, None), P("comp", "band", None, None)),
        check_vma=False,
    )
```

```python
import jax
import jax.numpy as jnp
from jax import lax
from jax.sharding import PartitionSpec as P
from jax.experimental import pallas as pl
from jax.experimental.pallas import tpu as pltpu

NF = 4
NSTEPS = 4
CAP = 4

COUPLING = 0.25
VERTICAL = 0.15
HIGHEST = lax.Precision.HIGHEST


def _advance_rows(src, dst, d_ref, r0, count, out_r0, bounds):
    lev, cols = src.shape[1], src.shape[2]
    fields = src[pl.ds(r0, count)]
    row_north = src[pl.ds(r0 - 1, count)]
    row_south = src[pl.ds(r0 + 1, count)]
    diff = d_ref[pl.ds(r0, count)]
    level = lax.broadcasted_iota(jnp.int32, (count, lev, cols), 1)
    col_east = pltpu.roll(fields, 1, 2)
    col_west = pltpu.roll(fields, cols - 1, 2)
    level_below = jnp.where(level == 0, fields, pltpu.roll(fields, 1, 1))
    level_above = jnp.where(level == lev - 1, fields, pltpu.roll(fields, lev - 1, 1))
    horizontal = row_north + row_south + col_east + col_west - 4.0 * fields
    new = fields + diff * horizontal + VERTICAL * (level_below + level_above - 2.0 * fields)
    if bounds is not None:
        row = r0 + lax.broadcasted_iota(jnp.int32, (count, 1, 1), 0)
        new = jnp.where((row >= bounds[0]) & (row < bounds[1]), new, 0.0)
    dst[pl.ds(out_r0, count)] = new


def _diffusion_kernel(bounds_ref, f_ref, d_ref, o_ref, buf_a, buf_b):
    total = f_ref.shape[0]
    rows = o_ref.shape[0]
    halo = (total - rows) // 2
    bounds = (bounds_ref[0], bounds_ref[1])
    chunk = 5 if (total - 2) % 5 == 0 else 1
    src = f_ref
    targets = (buf_a, buf_b)
    for step in range(NSTEPS - 1):
        dst = targets[step % 2]
        dst[0] = src[0]
        dst[total - 1] = src[total - 1]

        def one(i, carry, src=src, dst=dst):
            r0 = 1 + i * chunk
            _advance_rows(src, dst, d_ref, r0, chunk, r0, bounds)
            return carry

        lax.fori_loop(0, (total - 2) // chunk, one, 0)
        src = dst
    last = 8 if rows % 8 == 0 else 1

    def final(i, carry):
        _advance_rows(src, o_ref, d_ref, halo + i * last, last, i * last, None)
        return carry

    lax.fori_loop(0, rows // last, final, 0)


def diffuse(layer_temp, diffusivity):
    n_bands = lax.axis_size("band")
    band = lax.axis_index("band")
    rows = layer_temp.shape[1]
    lev = layer_temp.shape[2]
    cols = layer_temp.shape[3]
    halo = NSTEPS
    total = rows + 2 * halo
    comb = jnp.concatenate([layer_temp[0], diffusivity[0][:, None, :]], axis=1)
    forward = [(i, i + 1) for i in range(n_bands - 1)]
    backward = [(i + 1, i) for i in range(n_bands - 1)]
    above = lax.ppermute(comb[rows - halo:], "band", forward)
    below = lax.ppermute(comb[:halo], "band", backward)
    padded = jnp.concatenate([above, comb, below], axis=0)
    fields = padded[:, :lev]
    diff = padded[:, lev:]
    first = jnp.where(band == 0, halo, 0)
    stop = jnp.where(band == n_bands - 1, halo + rows, total)
    bounds = jnp.stack([first, stop]).astype(jnp.int32)
    return pl.pallas_call(
        _diffusion_kernel,
        out_shape=jax.ShapeDtypeStruct((rows, lev, cols), jnp.float32),
        in_specs=[
            pl.BlockSpec(memory_space=pltpu.SMEM),
            pl.BlockSpec(memory_space=pltpu.VMEM),
            pl.BlockSpec(memory_space=pltpu.VMEM),
        ],
        out_specs=pl.BlockSpec(memory_space=pltpu.VMEM),
        scratch_shapes=[pltpu.VMEM((total, lev, cols), jnp.float32)] * 2,
    )(bounds, fields, diff)


def body(layer_temp, diffusivity, owner_band, block_index, remap_blocks):
    n_sections = lax.axis_size("comp")
    n_bands = lax.axis_size("band")
    section = lax.axis_index("comp")
    rows = layer_temp.shape[1]
    cols = layer_temp.shape[3]
    width = NF * cols
    is_ocean = section == n_sections - 1
    weights_local = remap_blocks[0]

    surface_layers = layer_temp[0, :, :NF, :].astype(jnp.bfloat16)
    flux = lax.cond(
        is_ocean,
        lambda: jnp.zeros((rows, NF, cols), jnp.float32),
        lambda: jnp.einsum(
            "rfc,rcd->rfd", surface_layers, weights_local, preferred_element_type=jnp.float32
        ),
    )

    destination = owner_band[0, :, 0]
    dest_onehot = (destination[:, None] == jnp.arange(n_bands, dtype=jnp.int32)[None, :]).astype(
        jnp.float32
    )
    positions = jnp.arange(rows, dtype=jnp.int32)
    earlier_mask = (positions[:, None] > positions[None, :]).astype(jnp.float32)
    earlier = jnp.dot(earlier_mask, dest_onehot, precision=HIGHEST)
    slot_rank = jnp.sum(earlier * dest_onehot, axis=1).astype(jnp.int32)
    slot_onehot = (slot_rank[:, None] == jnp.arange(CAP, dtype=jnp.int32)[None, :]).astype(
        jnp.float32
    )
    selector = (dest_onehot[:, :, None] * slot_onehot[:, None, :]).reshape(rows, n_bands * CAP)

    index_lanes = jnp.broadcast_to(block_index[0].astype(jnp.float32)[:, None], (rows, 128))
    payload = jnp.concatenate([flux.reshape(rows, width), index_lanes], axis=1)
    sending = jnp.einsum("rk,rx->kx", selector, payload, precision=HIGHEST)
    sending = sending.reshape(n_bands, CAP, width + 128)
    received = lax.all_to_all(sending, "band", 0, 0, tiled=True)
    received = received.reshape(n_bands * CAP, width + 128)
    got_index = received[:, width].astype(jnp.int32)
    match = (got_index[:, None] == positions[None, :]).astype(jnp.float32)
    partial = jnp.einsum("kr,kx->rx", match, received[:, :width], precision=HIGHEST)
    last = n_sections - 1
    ocean_heat = partial
    for source in range(last):
        ocean_heat = ocean_heat + lax.ppermute(partial, "comp", [(source, last)])

    fields = diffuse(layer_temp, diffusivity)
    heating = jnp.where(is_ocean, COUPLING * ocean_heat, 0.0).reshape(rows, NF, cols)
    temp_out = fields.at[:, :NF].add(heating)
    sea_surface = temp_out[:, :NF].astype(jnp.bfloat16)
    returned = lax.cond(
        is_ocean,
        lambda: jnp.einsum(
            "rfc,rcd->rfd", sea_surface, weights_local, preferred_element_type=jnp.float32
        ).astype(jnp.bfloat16),
        lambda: jnp.zeros((rows, NF, cols), jnp.bfloat16),
    )

    ocean_rows = returned
    for target in range(last):
        ocean_rows = ocean_rows + lax.ppermute(returned, "comp", [(last, target)])
    ocean_rows = ocean_rows.reshape(rows, width)
    reply = jnp.einsum(
        "kr,rx->kx", match.astype(jnp.bfloat16), ocean_rows, preferred_element_type=jnp.float32
    ).astype(jnp.bfloat16)
    reply = reply.reshape(n_bands, CAP, width)
    came_back = lax.all_to_all(reply, "band", 0, 0, tiled=True)
    came_back = came_back.reshape(n_bands * CAP, width)
    seen = jnp.einsum(
        "rk,kx->rx", selector.astype(jnp.bfloat16), came_back, preferred_element_type=jnp.float32
    ).astype(jnp.bfloat16)
    surface_temp = jnp.where(is_ocean, returned, seen.reshape(rows, NF, cols))
    return temp_out[None], surface_temp[None]


def solution(mesh):
    return jax.shard_map(
        body,
        mesh=mesh,
        in_specs=(
            P("comp", "band", None, None),
            P("comp", "band", None),
            P("comp", "band", None),
            P("comp", "band"),
            P("comp", "band", None, None),
        ),
        out_specs=(P("comp", "band", None, None), P("comp", "band", None, None)),
        check_vma=False,
    )
```

```python
import jax
import jax.numpy as jnp
from jax import lax
from jax.sharding import PartitionSpec as P
from jax.experimental import pallas as pl
from jax.experimental.pallas import tpu as pltpu

NF = 4
NSTEPS = 4
CAP = 4

COUPLING = 0.25
VERTICAL = 0.15
HIGHEST = lax.Precision.HIGHEST
LINK = jnp.float16


def _advance_rows(src, dst, d_ref, r0, count, out_r0, bounds):
    lev, cols = src.shape[1], src.shape[2]
    fields = src[pl.ds(r0, count)]
    row_north = src[pl.ds(r0 - 1, count)]
    row_south = src[pl.ds(r0 + 1, count)]
    diff = d_ref[pl.ds(r0, count)]
    level = lax.broadcasted_iota(jnp.int32, (count, lev, cols), 1)
    col_east = pltpu.roll(fields, 1, 2)
    col_west = pltpu.roll(fields, cols - 1, 2)
    level_below = jnp.where(level == 0, fields, pltpu.roll(fields, 1, 1))
    level_above = jnp.where(level == lev - 1, fields, pltpu.roll(fields, lev - 1, 1))
    horizontal = row_north + row_south + col_east + col_west - 4.0 * fields
    new = fields + diff * horizontal + VERTICAL * (level_below + level_above - 2.0 * fields)
    if bounds is not None:
        row = r0 + lax.broadcasted_iota(jnp.int32, (count, 1, 1), 0)
        new = jnp.where((row >= bounds[0]) & (row < bounds[1]), new, 0.0)
    dst[pl.ds(out_r0, count)] = new


def _diffusion_kernel(bounds_ref, f_ref, d_ref, o_ref, buf_a, buf_b):
    total = f_ref.shape[0]
    rows = o_ref.shape[0]
    halo = (total - rows) // 2
    bounds = (bounds_ref[0], bounds_ref[1])
    chunk = 5 if (total - 2) % 5 == 0 else 1
    src = f_ref
    targets = (buf_a, buf_b)
    for step in range(NSTEPS - 1):
        dst = targets[step % 2]
        dst[0] = src[0]
        dst[total - 1] = src[total - 1]

        def one(i, carry, src=src, dst=dst):
            r0 = 1 + i * chunk
            _advance_rows(src, dst, d_ref, r0, chunk, r0, bounds)
            return carry

        lax.fori_loop(0, (total - 2) // chunk, one, 0)
        src = dst
    last = 8 if rows % 8 == 0 else 1

    def final(i, carry):
        _advance_rows(src, o_ref, d_ref, halo + i * last, last, i * last, None)
        return carry

    lax.fori_loop(0, rows // last, final, 0)


def diffuse(layer_temp, diffusivity):
    n_bands = lax.axis_size("band")
    band = lax.axis_index("band")
    rows = layer_temp.shape[1]
    lev = layer_temp.shape[2]
    cols = layer_temp.shape[3]
    halo = NSTEPS
    total = rows + 2 * halo
    comb = jnp.concatenate([layer_temp[0], diffusivity[0][:, None, :]], axis=1)
    forward = [(i, i + 1) for i in range(n_bands - 1)]
    backward = [(i + 1, i) for i in range(n_bands - 1)]
    above = lax.ppermute(comb[rows - halo:], "band", forward)
    below = lax.ppermute(comb[:halo], "band", backward)
    padded = jnp.concatenate([above, comb, below], axis=0)
    fields = padded[:, :lev]
    diff = padded[:, lev:]
    first = jnp.where(band == 0, halo, 0)
    stop = jnp.where(band == n_bands - 1, halo + rows, total)
    bounds = jnp.stack([first, stop]).astype(jnp.int32)
    return pl.pallas_call(
        _diffusion_kernel,
        out_shape=jax.ShapeDtypeStruct((rows, lev, cols), jnp.float32),
        in_specs=[
            pl.BlockSpec(memory_space=pltpu.SMEM),
            pl.BlockSpec(memory_space=pltpu.VMEM),
            pl.BlockSpec(memory_space=pltpu.VMEM),
        ],
        out_specs=pl.BlockSpec(memory_space=pltpu.VMEM),
        scratch_shapes=[pltpu.VMEM((total, lev, cols), jnp.float32)] * 2,
    )(bounds, fields, diff)


def body(layer_temp, diffusivity, owner_band, block_index, remap_blocks):
    n_sections = lax.axis_size("comp")
    n_bands = lax.axis_size("band")
    section = lax.axis_index("comp")
    rows = layer_temp.shape[1]
    cols = layer_temp.shape[3]
    width = NF * cols
    is_ocean = section == n_sections - 1
    weights_local = remap_blocks[0]

    surface_layers = layer_temp[0, :, :NF, :].astype(jnp.bfloat16)
    flux = lax.cond(
        is_ocean,
        lambda: jnp.zeros((rows, NF, cols), jnp.float32),
        lambda: jnp.einsum(
            "rfc,rcd->rfd", surface_layers, weights_local, preferred_element_type=jnp.float32
        ),
    )

    destination = owner_band[0, :, 0]
    dest_onehot = (destination[:, None] == jnp.arange(n_bands, dtype=jnp.int32)[None, :]).astype(
        jnp.float32
    )
    positions = jnp.arange(rows, dtype=jnp.int32)
    earlier_mask = (positions[:, None] > positions[None, :]).astype(jnp.float32)
    earlier = jnp.dot(earlier_mask, dest_onehot, precision=HIGHEST)
    slot_rank = jnp.sum(earlier * dest_onehot, axis=1).astype(jnp.int32)
    slot_onehot = (slot_rank[:, None] == jnp.arange(CAP, dtype=jnp.int32)[None, :]).astype(
        jnp.float32
    )
    selector = (dest_onehot[:, :, None] * slot_onehot[:, None, :]).reshape(rows, n_bands * CAP)

    index_lanes = jnp.broadcast_to(block_index[0].astype(jnp.float32)[:, None], (rows, 128))
    payload = jnp.concatenate([flux.reshape(rows, width), index_lanes], axis=1)
    sending = jnp.einsum("rk,rx->kx", selector, payload, precision=HIGHEST)
    sending = sending.reshape(n_bands, CAP, width + 128).astype(LINK)
    received = lax.all_to_all(sending, "band", 0, 0, tiled=True)
    received = received.reshape(n_bands * CAP, width + 128).astype(jnp.float32)
    got_index = received[:, width].astype(jnp.int32)
    match = (got_index[:, None] == positions[None, :]).astype(jnp.float32)
    partial = jnp.einsum("kr,kx->rx", match, received[:, :width], precision=HIGHEST)
    last = n_sections - 1
    scaled = (COUPLING * partial).astype(LINK)
    heating = scaled.astype(jnp.float32)
    for source in range(last):
        heating = heating + lax.ppermute(scaled, "comp", [(source, last)]).astype(jnp.float32)

    fields = diffuse(layer_temp, diffusivity)
    heating = jnp.where(is_ocean, heating, 0.0).reshape(rows, NF, cols)
    temp_out = fields.at[:, :NF].add(heating)
    sea_surface = temp_out[:, :NF].astype(jnp.bfloat16)
    returned = lax.cond(
        is_ocean,
        lambda: jnp.einsum(
            "rfc,rcd->rfd", sea_surface, weights_local, preferred_element_type=jnp.float32
        ).astype(jnp.bfloat16),
        lambda: jnp.zeros((rows, NF, cols), jnp.bfloat16),
    )

    ocean_rows = returned
    for target in range(last):
        ocean_rows = ocean_rows + lax.ppermute(returned, "comp", [(last, target)])
    ocean_rows = ocean_rows.reshape(rows, width)
    reply = jnp.einsum(
        "kr,rx->kx", match.astype(jnp.bfloat16), ocean_rows, preferred_element_type=jnp.float32
    ).astype(jnp.bfloat16)
    reply = reply.reshape(n_bands, CAP, width)
    came_back = lax.all_to_all(reply, "band", 0, 0, tiled=True)
    came_back = came_back.reshape(n_bands * CAP, width)
    seen = jnp.einsum(
        "rk,kx->rx", selector.astype(jnp.bfloat16), came_back, preferred_element_type=jnp.float32
    ).astype(jnp.bfloat16)
    surface_temp = jnp.where(is_ocean, returned, seen.reshape(rows, NF, cols))
    return temp_out[None], surface_temp[None]


def solution(mesh):
    return jax.shard_map(
        body,
        mesh=mesh,
        in_specs=(
            P("comp", "band", None, None),
            P("comp", "band", None),
            P("comp", "band", None),
            P("comp", "band"),
            P("comp", "band", None, None),
        ),
        out_specs=(P("comp", "band", None, None), P("comp", "band", None, None)),
        check_vma=False,
    )
```

```python
import jax
import jax.numpy as jnp
from jax import lax
from jax.sharding import PartitionSpec as P
from jax.experimental import pallas as pl
from jax.experimental.pallas import tpu as pltpu

NF = 4
NSTEPS = 4
CAP = 4

COUPLING = 0.25
VERTICAL = 0.15
HIGHEST = lax.Precision.HIGHEST
LINK = jnp.float16


def _advance_rows(src, dst, d_ref, r0, count, out_r0, bounds):
    lev, cols = src.shape[1], src.shape[2]
    fields = src[pl.ds(r0, count)]
    row_north = src[pl.ds(r0 - 1, count)]
    row_south = src[pl.ds(r0 + 1, count)]
    diff = d_ref[pl.ds(r0, count)]
    level = lax.broadcasted_iota(jnp.int32, (count, lev, cols), 1)
    col_east = pltpu.roll(fields, 1, 2)
    col_west = pltpu.roll(fields, cols - 1, 2)
    level_below = jnp.where(level == 0, fields, pltpu.roll(fields, 1, 1))
    level_above = jnp.where(level == lev - 1, fields, pltpu.roll(fields, lev - 1, 1))
    horizontal = row_north + row_south + col_east + col_west - 4.0 * fields
    new = fields + diff * horizontal + VERTICAL * (level_below + level_above - 2.0 * fields)
    if bounds is not None:
        row = r0 + lax.broadcasted_iota(jnp.int32, (count, 1, 1), 0)
        new = jnp.where((row >= bounds[0]) & (row < bounds[1]), new, 0.0)
    dst[pl.ds(out_r0, count)] = new


def _diffusion_kernel(bounds_ref, f_ref, d_ref, o_ref, buf_a, buf_b):
    total = f_ref.shape[0]
    rows = o_ref.shape[0]
    halo = (total - rows) // 2
    bounds = (bounds_ref[0], bounds_ref[1])
    chunk = 5 if (total - 2) % 5 == 0 else 1
    src = f_ref
    targets = (buf_a, buf_b)
    for step in range(NSTEPS - 1):
        dst = targets[step % 2]
        dst[0] = src[0]
        dst[total - 1] = src[total - 1]

        def one(i, carry, src=src, dst=dst):
            r0 = 1 + i * chunk
            _advance_rows(src, dst, d_ref, r0, chunk, r0, bounds)
            return carry

        lax.fori_loop(0, (total - 2) // chunk, one, 0)
        src = dst
    last = 8 if rows % 8 == 0 else 1

    def final(i, carry):
        _advance_rows(src, o_ref, d_ref, halo + i * last, last, i * last, None)
        return carry

    lax.fori_loop(0, rows // last, final, 0)


def exchange_halo(layer_temp, diffusivity):
    n_bands = lax.axis_size("band")
    band = lax.axis_index("band")
    rows = layer_temp.shape[1]
    lev = layer_temp.shape[2]
    halo = NSTEPS
    total = rows + 2 * halo
    comb = jnp.concatenate([layer_temp[0], diffusivity[0][:, None, :]], axis=1)
    forward = [(i, i + 1) for i in range(n_bands - 1)]
    backward = [(i + 1, i) for i in range(n_bands - 1)]
    above = lax.ppermute(comb[rows - halo:], "band", forward)
    below = lax.ppermute(comb[:halo], "band", backward)
    padded = jnp.concatenate([above, comb, below], axis=0)
    first = jnp.where(band == 0, halo, 0)
    stop = jnp.where(band == n_bands - 1, halo + rows, total)
    bounds = jnp.stack([first, stop]).astype(jnp.int32)
    return padded, bounds


def diffuse(padded, bounds, lev):
    total, _, cols = padded.shape
    rows = total - 2 * NSTEPS
    fields = padded[:, :lev]
    diff = padded[:, lev:]
    return pl.pallas_call(
        _diffusion_kernel,
        out_shape=jax.ShapeDtypeStruct((rows, lev, cols), jnp.float32),
        in_specs=[
            pl.BlockSpec(memory_space=pltpu.SMEM),
            pl.BlockSpec(memory_space=pltpu.VMEM),
            pl.BlockSpec(memory_space=pltpu.VMEM),
        ],
        out_specs=pl.BlockSpec(memory_space=pltpu.VMEM),
        scratch_shapes=[pltpu.VMEM((total, lev, cols), jnp.float32)] * 2,
    )(bounds, fields, diff)


def body(layer_temp, diffusivity, owner_band, block_index, remap_blocks):
    n_sections = lax.axis_size("comp")
    n_bands = lax.axis_size("band")
    section = lax.axis_index("comp")
    rows = layer_temp.shape[1]
    cols = layer_temp.shape[3]
    width = NF * cols
    is_ocean = section == n_sections - 1
    weights_local = remap_blocks[0]

    lev = layer_temp.shape[2]
    padded, bounds = exchange_halo(layer_temp, diffusivity)
    surface_layers = layer_temp[0, :, :NF, :].astype(jnp.bfloat16)
    flux, fields_early = lax.cond(
        is_ocean,
        lambda: (jnp.zeros((rows, NF, cols), jnp.float32), diffuse(padded, bounds, lev)),
        lambda: (
            jnp.einsum(
                "rfc,rcd->rfd", surface_layers, weights_local, preferred_element_type=jnp.float32
            ),
            jnp.zeros((rows, lev, cols), jnp.float32),
        ),
    )

    destination = owner_band[0, :, 0]
    dest_onehot = (destination[:, None] == jnp.arange(n_bands, dtype=jnp.int32)[None, :]).astype(
        jnp.float32
    )
    positions = jnp.arange(rows, dtype=jnp.int32)
    earlier_mask = (positions[:, None] > positions[None, :]).astype(jnp.float32)
    earlier = jnp.dot(earlier_mask, dest_onehot, precision=HIGHEST)
    slot_rank = jnp.sum(earlier * dest_onehot, axis=1).astype(jnp.int32)
    slot_onehot = (slot_rank[:, None] == jnp.arange(CAP, dtype=jnp.int32)[None, :]).astype(
        jnp.float32
    )
    selector = (dest_onehot[:, :, None] * slot_onehot[:, None, :]).reshape(rows, n_bands * CAP)

    index_lanes = jnp.broadcast_to(block_index[0].astype(jnp.float32)[:, None], (rows, 128))
    payload = jnp.concatenate([flux.reshape(rows, width), index_lanes], axis=1)
    sending = jnp.einsum("rk,rx->kx", selector, payload, precision=HIGHEST)
    sending = sending.reshape(n_bands, CAP, width + 128).astype(LINK)
    received = lax.all_to_all(sending, "band", 0, 0, tiled=True)
    received = received.reshape(n_bands * CAP, width + 128).astype(jnp.float32)
    got_index = received[:, width].astype(jnp.int32)
    match = (got_index[:, None] == positions[None, :]).astype(jnp.float32)
    partial = jnp.einsum("kr,kx->rx", match, received[:, :width], precision=HIGHEST)
    last = n_sections - 1
    scaled = (COUPLING * partial).astype(LINK)
    heating = scaled.astype(jnp.float32)
    for source in range(last):
        heating = heating + lax.ppermute(scaled, "comp", [(source, last)]).astype(jnp.float32)

    padded_late, _ = lax.optimization_barrier((padded, scaled))
    fields = lax.cond(
        is_ocean, lambda: fields_early, lambda: diffuse(padded_late, bounds, lev)
    )
    heating = jnp.where(is_ocean, heating, 0.0).reshape(rows, NF, cols)
    temp_out = fields.at[:, :NF].add(heating)
    sea_surface = temp_out[:, :NF].astype(jnp.bfloat16)
    returned = lax.cond(
        is_ocean,
        lambda: jnp.einsum(
            "rfc,rcd->rfd", sea_surface, weights_local, preferred_element_type=jnp.float32
        ).astype(jnp.bfloat16),
        lambda: jnp.zeros((rows, NF, cols), jnp.bfloat16),
    )

    ocean_rows = returned
    for target in range(last):
        ocean_rows = ocean_rows + lax.ppermute(returned, "comp", [(last, target)])
    ocean_rows = ocean_rows.reshape(rows, width)
    reply = jnp.einsum(
        "kr,rx->kx", match.astype(jnp.bfloat16), ocean_rows, preferred_element_type=jnp.float32
    ).astype(jnp.bfloat16)
    reply = reply.reshape(n_bands, CAP, width)
    came_back = lax.all_to_all(reply, "band", 0, 0, tiled=True)
    came_back = came_back.reshape(n_bands * CAP, width)
    seen = jnp.einsum(
        "rk,kx->rx", selector.astype(jnp.bfloat16), came_back, preferred_element_type=jnp.float32
    ).astype(jnp.bfloat16)
    surface_temp = jnp.where(is_ocean, returned, seen.reshape(rows, NF, cols))
    return temp_out[None], surface_temp[None]


def solution(mesh):
    return jax.shard_map(
        body,
        mesh=mesh,
        in_specs=(
            P("comp", "band", None, None),
            P("comp", "band", None),
            P("comp", "band", None),
            P("comp", "band"),
            P("comp", "band", None, None),
        ),
        out_specs=(P("comp", "band", None, None), P("comp", "band", None, None)),
        check_vma=False,
    )
```

```python
import jax
import jax.numpy as jnp
from jax import lax
from jax.sharding import PartitionSpec as P
from jax.experimental import pallas as pl
from jax.experimental.pallas import tpu as pltpu

NF = 4
NSTEPS = 4
CAP = 4

COUPLING = 0.25
VERTICAL = 0.15
HIGHEST = lax.Precision.HIGHEST
LINK = jnp.float16


def _advance_rows(src, dst, d_ref, r0, count, out_r0, bounds):
    lev, cols = dst.shape[1], dst.shape[2]
    fields = src[pl.ds(r0, count), pl.ds(0, lev)]
    row_north = src[pl.ds(r0 - 1, count), pl.ds(0, lev)]
    row_south = src[pl.ds(r0 + 1, count), pl.ds(0, lev)]
    diff = d_ref[pl.ds(r0, count), pl.ds(lev, 1)]
    level = lax.broadcasted_iota(jnp.int32, (count, lev, cols), 1)
    col_east = pltpu.roll(fields, 1, 2)
    col_west = pltpu.roll(fields, cols - 1, 2)
    level_below = jnp.where(level == 0, fields, pltpu.roll(fields, 1, 1))
    level_above = jnp.where(level == lev - 1, fields, pltpu.roll(fields, lev - 1, 1))
    horizontal = row_north + row_south + col_east + col_west - 4.0 * fields
    new = fields + diff * horizontal + VERTICAL * (level_below + level_above - 2.0 * fields)
    if bounds is not None:
        row = r0 + lax.broadcasted_iota(jnp.int32, (count, 1, 1), 0)
        new = jnp.where((row >= bounds[0]) & (row < bounds[1]), new, 0.0)
    dst[pl.ds(out_r0, count)] = new


def _largest_divisor(n, limit):
    return max(k for k in range(1, limit + 1) if n % k == 0)


def _diffusion_kernel(bounds_ref, p_ref, o_ref, buf_a, buf_b):
    total = p_ref.shape[0]
    rows, lev = o_ref.shape[0], o_ref.shape[1]
    halo = (total - rows) // 2
    bounds = (bounds_ref[0], bounds_ref[1])
    chunk = _largest_divisor(total - 2, 16)
    src = p_ref
    targets = (buf_a, buf_b)
    for step in range(NSTEPS - 1):
        dst = targets[step % 2]
        dst[0] = src[0, pl.ds(0, lev)]
        dst[total - 1] = src[total - 1, pl.ds(0, lev)]

        def one(i, carry, src=src, dst=dst):
            r0 = 1 + i * chunk
            _advance_rows(src, dst, p_ref, r0, chunk, r0, bounds)
            return carry

        lax.fori_loop(0, (total - 2) // chunk, one, 0)
        src = dst
    last = _largest_divisor(rows, 16)

    def final(i, carry):
        _advance_rows(src, o_ref, p_ref, halo + i * last, last, i * last, None)
        return carry

    lax.fori_loop(0, rows // last, final, 0)


def diffuse(layer_temp, diffusivity):
    n_bands = lax.axis_size("band")
    band = lax.axis_index("band")
    rows = layer_temp.shape[1]
    lev = layer_temp.shape[2]
    cols = layer_temp.shape[3]
    halo = NSTEPS
    total = rows + 2 * halo
    comb = jnp.concatenate([layer_temp[0], diffusivity[0][:, None, :]], axis=1)
    forward = [(i, i + 1) for i in range(n_bands - 1)]
    backward = [(i + 1, i) for i in range(n_bands - 1)]
    above = lax.ppermute(comb[rows - halo:], "band", forward)
    below = lax.ppermute(comb[:halo], "band", backward)
    padded = jnp.concatenate([above, comb, below], axis=0)
    first = jnp.where(band == 0, halo, 0)
    stop = jnp.where(band == n_bands - 1, halo + rows, total)
    bounds = jnp.stack([first, stop]).astype(jnp.int32)
    return pl.pallas_call(
        _diffusion_kernel,
        out_shape=jax.ShapeDtypeStruct((rows, lev, cols), jnp.float32),
        in_specs=[
            pl.BlockSpec(memory_space=pltpu.SMEM),
            pl.BlockSpec(memory_space=pltpu.VMEM),
        ],
        out_specs=pl.BlockSpec(memory_space=pltpu.VMEM),
        scratch_shapes=[pltpu.VMEM((total, lev, cols), jnp.float32)] * 2,
    )(bounds, padded)


def body(layer_temp, diffusivity, owner_band, block_index, remap_blocks):
    n_sections = lax.axis_size("comp")
    n_bands = lax.axis_size("band")
    section = lax.axis_index("comp")
    rows = layer_temp.shape[1]
    cols = layer_temp.shape[3]
    width = NF * cols
    is_ocean = section == n_sections - 1
    weights_local = remap_blocks[0]

    surface_layers = layer_temp[0, :, :NF, :].astype(jnp.bfloat16)
    flux = lax.cond(
        is_ocean,
        lambda: jnp.zeros((rows, NF, cols), jnp.float32),
        lambda: jnp.einsum(
            "rfc,rcd->rfd", surface_layers, weights_local, preferred_element_type=jnp.float32
        ),
    )

    destination = owner_band[0, :, 0]
    dest_onehot = (destination[:, None] == jnp.arange(n_bands, dtype=jnp.int32)[None, :]).astype(
        jnp.float32
    )
    positions = jnp.arange(rows, dtype=jnp.int32)
    earlier_mask = (positions[:, None] > positions[None, :]).astype(jnp.float32)
    earlier = jnp.dot(earlier_mask, dest_onehot, precision=HIGHEST)
    slot_rank = jnp.sum(earlier * dest_onehot, axis=1).astype(jnp.int32)
    slot_onehot = (slot_rank[:, None] == jnp.arange(CAP, dtype=jnp.int32)[None, :]).astype(
        jnp.float32
    )
    selector = (dest_onehot[:, :, None] * slot_onehot[:, None, :]).reshape(rows, n_bands * CAP)

    index_lanes = jnp.broadcast_to(block_index[0].astype(jnp.float32)[:, None], (rows, 128))
    payload = jnp.concatenate([flux.reshape(rows, width), index_lanes], axis=1)
    sending = jnp.einsum("rk,rx->kx", selector, payload, precision=HIGHEST)
    sending = sending.reshape(n_bands, CAP, width + 128).astype(LINK)
    received = lax.all_to_all(sending, "band", 0, 0, tiled=True)
    received = received.reshape(n_bands * CAP, width + 128).astype(jnp.float32)
    got_index = received[:, width].astype(jnp.int32)
    match = (got_index[:, None] == positions[None, :]).astype(jnp.float32)
    partial = jnp.einsum("kr,kx->rx", match, received[:, :width], precision=HIGHEST)
    last = n_sections - 1
    scaled = (COUPLING * partial).astype(LINK)
    heating = scaled.astype(jnp.float32)
    for source in range(last):
        heating = heating + lax.ppermute(scaled, "comp", [(source, last)]).astype(jnp.float32)

    fields = diffuse(layer_temp, diffusivity)
    heating = jnp.where(is_ocean, heating, 0.0).reshape(rows, NF, cols)
    temp_out = fields.at[:, :NF].add(heating)
    sea_surface = temp_out[:, :NF].astype(jnp.bfloat16)
    returned = lax.cond(
        is_ocean,
        lambda: jnp.einsum(
            "rfc,rcd->rfd", sea_surface, weights_local, preferred_element_type=jnp.float32
        ).astype(jnp.bfloat16),
        lambda: jnp.zeros((rows, NF, cols), jnp.bfloat16),
    )

    ocean_rows = returned
    for target in range(last):
        ocean_rows = ocean_rows + lax.ppermute(returned, "comp", [(last, target)])
    ocean_rows = ocean_rows.reshape(rows, width)
    reply = jnp.einsum(
        "kr,rx->kx", match.astype(jnp.bfloat16), ocean_rows, preferred_element_type=jnp.float32
    ).astype(jnp.bfloat16)
    reply = reply.reshape(n_bands, CAP, width)
    came_back = lax.all_to_all(reply, "band", 0, 0, tiled=True)
    came_back = came_back.reshape(n_bands * CAP, width)
    seen = jnp.einsum(
        "rk,kx->rx", selector.astype(jnp.bfloat16), came_back, preferred_element_type=jnp.float32
    ).astype(jnp.bfloat16)
    surface_temp = jnp.where(is_ocean, returned, seen.reshape(rows, NF, cols))
    return temp_out[None], surface_temp[None]


def solution(mesh):
    return jax.shard_map(
        body,
        mesh=mesh,
        in_specs=(
            P("comp", "band", None, None),
            P("comp", "band", None),
            P("comp", "band", None),
            P("comp", "band"),
            P("comp", "band", None, None),
        ),
        out_specs=(P("comp", "band", None, None), P("comp", "band", None, None)),
        check_vma=False,
    )
```

```python
import jax
import jax.numpy as jnp
from jax import lax
from jax.sharding import PartitionSpec as P
from jax.experimental import pallas as pl
from jax.experimental.pallas import tpu as pltpu

NF = 4
NSTEPS = 4
CAP = 4

COUPLING = 0.25
VERTICAL = 0.15
HIGHEST = lax.Precision.HIGHEST
LINK = jnp.float16


def _advance_rows(src, dst, d_ref, r0, count, out_r0, bounds):
    lev, cols = dst.shape[1], dst.shape[2]
    fields = src[pl.ds(r0, count), pl.ds(0, lev)]
    row_north = src[pl.ds(r0 - 1, count), pl.ds(0, lev)]
    row_south = src[pl.ds(r0 + 1, count), pl.ds(0, lev)]
    diff = d_ref[pl.ds(r0, count), pl.ds(lev, 1)]
    level = lax.broadcasted_iota(jnp.int32, (count, lev, cols), 1)
    col_east = pltpu.roll(fields, 1, 2)
    col_west = pltpu.roll(fields, cols - 1, 2)
    level_below = jnp.where(level == 0, fields, pltpu.roll(fields, 1, 1))
    level_above = jnp.where(level == lev - 1, fields, pltpu.roll(fields, lev - 1, 1))
    horizontal = row_north + row_south + col_east + col_west - 4.0 * fields
    new = fields + diff * horizontal + VERTICAL * (level_below + level_above - 2.0 * fields)
    if bounds is not None:
        row = r0 + lax.broadcasted_iota(jnp.int32, (count, 1, 1), 0)
        new = jnp.where((row >= bounds[0]) & (row < bounds[1]), new, 0.0)
    dst[pl.ds(out_r0, count)] = new


def _largest_divisor(n, limit):
    return max(k for k in range(1, limit + 1) if n % k == 0)


def _diffusion_kernel(bounds_ref, p_ref, o_ref, buf_a, buf_b):
    total = p_ref.shape[0]
    rows, lev = o_ref.shape[0], o_ref.shape[1]
    halo = (total - rows) // 2
    bounds = (bounds_ref[0], bounds_ref[1])
    chunk = _largest_divisor(total - 2, 16)
    src = p_ref
    targets = (buf_a, buf_b)
    for step in range(NSTEPS - 1):
        dst = targets[step % 2]
        dst[0] = src[0, pl.ds(0, lev)]
        dst[total - 1] = src[total - 1, pl.ds(0, lev)]

        def one(i, carry, src=src, dst=dst):
            r0 = 1 + i * chunk
            _advance_rows(src, dst, p_ref, r0, chunk, r0, bounds)
            return carry

        lax.fori_loop(0, (total - 2) // chunk, one, 0)
        src = dst
    last = _largest_divisor(rows, 16)

    def final(i, carry):
        _advance_rows(src, o_ref, p_ref, halo + i * last, last, i * last, None)
        return carry

    lax.fori_loop(0, rows // last, final, 0)


def diffuse(layer_temp, diffusivity):
    n_bands = lax.axis_size("band")
    band = lax.axis_index("band")
    rows = layer_temp.shape[1]
    lev = layer_temp.shape[2]
    cols = layer_temp.shape[3]
    halo = NSTEPS
    total = rows + 2 * halo
    comb = jnp.concatenate([layer_temp[0], diffusivity[0][:, None, :]], axis=1)
    forward = [(i, i + 1) for i in range(n_bands - 1)]
    backward = [(i + 1, i) for i in range(n_bands - 1)]
    above = lax.ppermute(comb[rows - halo:], "band", forward)
    below = lax.ppermute(comb[:halo], "band", backward)
    padded = jnp.concatenate([above, comb, below], axis=0)
    first = jnp.where(band == 0, halo, 0)
    stop = jnp.where(band == n_bands - 1, halo + rows, total)
    bounds = jnp.stack([first, stop]).astype(jnp.int32)
    return pl.pallas_call(
        _diffusion_kernel,
        out_shape=jax.ShapeDtypeStruct((rows, lev, cols), jnp.float32),
        in_specs=[
            pl.BlockSpec(memory_space=pltpu.SMEM),
            pl.BlockSpec(memory_space=pltpu.VMEM),
        ],
        out_specs=pl.BlockSpec(memory_space=pltpu.VMEM),
        scratch_shapes=[pltpu.VMEM((total, lev, cols), jnp.float32)] * 2,
    )(bounds, padded)


def body(layer_temp, diffusivity, owner_band, block_index, remap_blocks):
    n_sections = lax.axis_size("comp")
    n_bands = lax.axis_size("band")
    section = lax.axis_index("comp")
    rows = layer_temp.shape[1]
    cols = layer_temp.shape[3]
    width = NF * cols
    is_ocean = section == n_sections - 1
    weights_local = remap_blocks[0]

    surface_layers = layer_temp[0, :, :NF, :].astype(jnp.bfloat16)
    flux = lax.cond(
        is_ocean,
        lambda: jnp.zeros((rows, NF, cols), jnp.float32),
        lambda: jnp.einsum(
            "rfc,rcd->rfd", surface_layers, weights_local, preferred_element_type=jnp.float32
        ),
    )

    destination = owner_band[0, :, 0]
    dest_onehot = (destination[:, None] == jnp.arange(n_bands, dtype=jnp.int32)[None, :]).astype(
        jnp.float32
    )
    positions = jnp.arange(rows, dtype=jnp.int32)
    earlier_mask = (positions[:, None] > positions[None, :]).astype(jnp.float32)
    earlier = jnp.dot(earlier_mask, dest_onehot, precision=HIGHEST)
    slot_rank = jnp.sum(earlier * dest_onehot, axis=1).astype(jnp.int32)
    slot_onehot = (slot_rank[:, None] == jnp.arange(CAP, dtype=jnp.int32)[None, :]).astype(
        jnp.float32
    )
    selector = dest_onehot[:, :, None] * slot_onehot[:, None, :]
    chunk = width + 128

    index_lanes = jnp.broadcast_to(block_index[0].astype(jnp.float32)[:, None], (rows, 128))
    payload = jnp.concatenate([flux.reshape(rows, width), index_lanes], axis=1)
    sending = jnp.concatenate(
        [
            jnp.einsum("rb,rx->bx", selector[:, :, k], payload, precision=HIGHEST)
            for k in range(CAP)
        ],
        axis=1,
    ).astype(LINK)
    received = lax.all_to_all(sending, "band", 0, 0, tiled=True).astype(jnp.float32)
    matches = []
    partial = None
    for k in range(CAP):
        got_index = received[:, k * chunk + width].astype(jnp.int32)
        match = (got_index[:, None] == positions[None, :]).astype(jnp.float32)
        matches.append(match)
        term = jnp.einsum(
            "br,bx->rx", match, received[:, k * chunk:k * chunk + width], precision=HIGHEST
        )
        partial = term if partial is None else partial + term
    last = n_sections - 1
    scaled = (COUPLING * partial).astype(LINK)
    heating = scaled.astype(jnp.float32)
    for source in range(last):
        heating = heating + lax.ppermute(scaled, "comp", [(source, last)]).astype(jnp.float32)

    fields = diffuse(layer_temp, diffusivity)
    heating = jnp.where(is_ocean, heating, 0.0).reshape(rows, NF, cols)
    sea_surface = (fields[:, :NF] + heating).astype(jnp.bfloat16)
    temp_out = fields.at[:, :NF].add(heating)
    returned = lax.cond(
        is_ocean,
        lambda: jnp.einsum(
            "rfc,rcd->rfd", sea_surface, weights_local, preferred_element_type=jnp.float32
        ).astype(jnp.bfloat16),
        lambda: jnp.zeros((rows, NF, cols), jnp.bfloat16),
    )

    ocean_rows = returned
    for target in range(last):
        ocean_rows = ocean_rows + lax.ppermute(returned, "comp", [(last, target)])
    ocean_rows = ocean_rows.reshape(rows, width)
    reply = jnp.concatenate(
        [
            jnp.einsum(
                "br,rx->bx",
                match.astype(jnp.bfloat16),
                ocean_rows,
                preferred_element_type=jnp.float32,
            ).astype(jnp.bfloat16)
            for match in matches
        ],
        axis=1,
    )
    came_back = lax.all_to_all(reply, "band", 0, 0, tiled=True)
    seen = None
    for k in range(CAP):
        term = jnp.einsum(
            "rb,bx->rx",
            selector[:, :, k].astype(jnp.bfloat16),
            came_back[:, k * width:(k + 1) * width],
            preferred_element_type=jnp.float32,
        )
        seen = term if seen is None else seen + term
    seen = seen.astype(jnp.bfloat16)
    surface_temp = jnp.where(is_ocean, returned, seen.reshape(rows, NF, cols))
    return temp_out[None], surface_temp[None]


def solution(mesh):
    return jax.shard_map(
        body,
        mesh=mesh,
        in_specs=(
            P("comp", "band", None, None),
            P("comp", "band", None),
            P("comp", "band", None),
            P("comp", "band"),
            P("comp", "band", None, None),
        ),
        out_specs=(P("comp", "band", None, None), P("comp", "band", None, None)),
        check_vma=False,
    )
```

```python
import jax
import jax.numpy as jnp
from jax import lax
from jax.sharding import PartitionSpec as P
from jax.experimental import pallas as pl
from jax.experimental.pallas import tpu as pltpu

NF = 4
NSTEPS = 4
CAP = 4

COUPLING = 0.25
VERTICAL = 0.15
HIGHEST = lax.Precision.HIGHEST
LINK = jnp.float16


def _advance_rows(src, dst, d_ref, r0, count, out_r0, bounds):
    lev, cols = dst.shape[1], dst.shape[2]
    fields = src[pl.ds(r0, count), pl.ds(0, lev)]
    row_north = src[pl.ds(r0 - 1, count), pl.ds(0, lev)]
    row_south = src[pl.ds(r0 + 1, count), pl.ds(0, lev)]
    diff = d_ref[pl.ds(r0, count), pl.ds(lev, 1)]
    level = lax.broadcasted_iota(jnp.int32, (count, lev, cols), 1)
    col_east = pltpu.roll(fields, 1, 2)
    col_west = pltpu.roll(fields, cols - 1, 2)
    level_below = jnp.where(level == 0, fields, pltpu.roll(fields, 1, 1))
    level_above = jnp.where(level == lev - 1, fields, pltpu.roll(fields, lev - 1, 1))
    horizontal = row_north + row_south + col_east + col_west - 4.0 * fields
    new = fields + diff * horizontal + VERTICAL * (level_below + level_above - 2.0 * fields)
    if bounds is not None:
        row = r0 + lax.broadcasted_iota(jnp.int32, (count, 1, 1), 0)
        new = jnp.where((row >= bounds[0]) & (row < bounds[1]), new, 0.0)
    dst[pl.ds(out_r0, count)] = new


def _largest_divisor(n, limit):
    return max(k for k in range(1, limit + 1) if n % k == 0)


def _diffusion_kernel(bounds_ref, p_ref, o_ref, buf_a, buf_b):
    total = p_ref.shape[0]
    rows, lev = o_ref.shape[0], o_ref.shape[1]
    halo = (total - rows) // 2
    bounds = (bounds_ref[0], bounds_ref[1])
    chunk = _largest_divisor(total - 2, 16)
    src = p_ref
    targets = (buf_a, buf_b)
    for step in range(NSTEPS - 1):
        dst = targets[step % 2]
        dst[0] = src[0, pl.ds(0, lev)]
        dst[total - 1] = src[total - 1, pl.ds(0, lev)]

        def one(i, carry, src=src, dst=dst):
            r0 = 1 + i * chunk
            _advance_rows(src, dst, p_ref, r0, chunk, r0, bounds)
            return carry

        lax.fori_loop(0, (total - 2) // chunk, one, 0)
        src = dst
    last = _largest_divisor(rows, 16)

    def final(i, carry):
        _advance_rows(src, o_ref, p_ref, halo + i * last, last, i * last, None)
        return carry

    lax.fori_loop(0, rows // last, final, 0)


def diffuse(layer_temp, diffusivity):
    n_bands = lax.axis_size("band")
    band = lax.axis_index("band")
    rows = layer_temp.shape[1]
    lev = layer_temp.shape[2]
    cols = layer_temp.shape[3]
    halo = NSTEPS
    total = rows + 2 * halo
    comb = jnp.concatenate([layer_temp[0], diffusivity[0][:, None, :]], axis=1)
    forward = [(i, i + 1) for i in range(n_bands - 1)]
    backward = [(i + 1, i) for i in range(n_bands - 1)]
    above = lax.ppermute(comb[rows - halo:], "band", forward)
    below = lax.ppermute(comb[:halo], "band", backward)
    padded = jnp.concatenate([above, comb, below], axis=0)
    first = jnp.where(band == 0, halo, 0)
    stop = jnp.where(band == n_bands - 1, halo + rows, total)
    bounds = jnp.stack([first, stop]).astype(jnp.int32)
    return pl.pallas_call(
        _diffusion_kernel,
        out_shape=jax.ShapeDtypeStruct((rows, lev, cols), jnp.float32),
        in_specs=[
            pl.BlockSpec(memory_space=pltpu.SMEM),
            pl.BlockSpec(memory_space=pltpu.VMEM),
        ],
        out_specs=pl.BlockSpec(memory_space=pltpu.VMEM),
        scratch_shapes=[pltpu.VMEM((total, lev, cols), jnp.float32)] * 2,
    )(bounds, padded)


def body(layer_temp, diffusivity, owner_band, block_index, remap_blocks):
    n_sections = lax.axis_size("comp")
    n_bands = lax.axis_size("band")
    section = lax.axis_index("comp")
    rows = layer_temp.shape[1]
    cols = layer_temp.shape[3]
    width = NF * cols
    is_ocean = section == n_sections - 1
    weights_local = remap_blocks[0]

    surface_layers = layer_temp[0, :, :NF, :].astype(jnp.bfloat16)
    flux = lax.cond(
        is_ocean,
        lambda: jnp.zeros((rows, NF, cols), jnp.float32),
        lambda: jnp.einsum(
            "rfc,rcd->rfd", surface_layers, weights_local, preferred_element_type=jnp.float32
        ),
    )

    destination = owner_band[0, :, 0]
    dest_onehot = (destination[:, None] == jnp.arange(n_bands, dtype=jnp.int32)[None, :]).astype(
        jnp.float32
    )
    positions = jnp.arange(rows, dtype=jnp.int32)
    earlier_mask = (positions[:, None] > positions[None, :]).astype(jnp.float32)
    earlier = jnp.dot(
        earlier_mask.astype(jnp.bfloat16),
        dest_onehot.astype(jnp.bfloat16),
        preferred_element_type=jnp.float32,
    )
    slot_rank = jnp.sum(earlier * dest_onehot, axis=1).astype(jnp.int32)
    slot_onehot = (slot_rank[:, None] == jnp.arange(CAP, dtype=jnp.int32)[None, :]).astype(
        jnp.float32
    )
    selector = (dest_onehot[:, :, None] * slot_onehot[:, None, :]).reshape(rows, n_bands * CAP)

    index_lanes = jnp.broadcast_to(block_index[0].astype(jnp.float32)[:, None], (rows, 128))
    payload = jnp.concatenate([flux.reshape(rows, width), index_lanes], axis=1)
    sending = jnp.einsum("rk,rx->kx", selector, payload, precision=HIGHEST)
    sending = sending.reshape(n_bands, CAP, width + 128).astype(LINK)
    received = lax.all_to_all(sending, "band", 0, 0, tiled=True)
    received = received.reshape(n_bands * CAP, width + 128).astype(jnp.float32)
    got_index = received[:, width].astype(jnp.int32)
    match = (got_index[:, None] == positions[None, :]).astype(jnp.float32)
    partial = jnp.einsum("kr,kx->rx", match, received[:, :width], precision=HIGHEST)
    last = n_sections - 1
    scaled = (COUPLING * partial).astype(LINK)
    heating = scaled.astype(jnp.float32)
    for source in range(last):
        heating = heating + lax.ppermute(scaled, "comp", [(source, last)]).astype(jnp.float32)

    fields = diffuse(layer_temp, diffusivity)
    heating = jnp.where(is_ocean, heating, 0.0).reshape(rows, NF, cols)
    temp_out = fields.at[:, :NF].add(heating)
    sea_surface = temp_out[:, :NF].astype(jnp.bfloat16)
    returned = lax.cond(
        is_ocean,
        lambda: jnp.einsum(
            "rfc,rcd->rfd", sea_surface, weights_local, preferred_element_type=jnp.float32
        ).astype(jnp.bfloat16),
        lambda: jnp.zeros((rows, NF, cols), jnp.bfloat16),
    )

    ocean_rows = returned
    for target in range(last):
        ocean_rows = ocean_rows + lax.ppermute(returned, "comp", [(last, target)])
    ocean_rows = ocean_rows.reshape(rows, width)
    reply = jnp.einsum(
        "kr,rx->kx", match.astype(jnp.bfloat16), ocean_rows, preferred_element_type=jnp.float32
    ).astype(jnp.bfloat16)
    reply = reply.reshape(n_bands, CAP, width)
    came_back = lax.all_to_all(reply, "band", 0, 0, tiled=True)
    came_back = came_back.reshape(n_bands * CAP, width)
    seen = jnp.einsum(
        "rk,kx->rx", selector.astype(jnp.bfloat16), came_back, preferred_element_type=jnp.float32
    ).astype(jnp.bfloat16)
    surface_temp = jnp.where(is_ocean, returned, seen.reshape(rows, NF, cols))
    return temp_out[None], surface_temp[None]


def solution(mesh):
    return jax.shard_map(
        body,
        mesh=mesh,
        in_specs=(
            P("comp", "band", None, None),
            P("comp", "band", None),
            P("comp", "band", None),
            P("comp", "band"),
            P("comp", "band", None, None),
        ),
        out_specs=(P("comp", "band", None, None), P("comp", "band", None, None)),
        check_vma=False,
    )
```

```python
import jax
import jax.numpy as jnp
from jax import lax
from jax.sharding import PartitionSpec as P
from jax.experimental import pallas as pl
from jax.experimental.pallas import tpu as pltpu

NF = 4
NSTEPS = 4
CAP = 4

COUPLING = 0.25
VERTICAL = 0.15
HIGHEST = lax.Precision.HIGHEST
LINK = jnp.float16


def _advance_rows(src, dst, d_ref, r0, count, out_r0, bounds):
    lev, cols = dst.shape[1], dst.shape[2]
    fields = src[pl.ds(r0, count), pl.ds(0, lev)]
    row_north = src[pl.ds(r0 - 1, count), pl.ds(0, lev)]
    row_south = src[pl.ds(r0 + 1, count), pl.ds(0, lev)]
    diff = d_ref[pl.ds(r0, count), pl.ds(lev, 1)]
    level = lax.broadcasted_iota(jnp.int32, (count, lev, cols), 1)
    col_east = pltpu.roll(fields, 1, 2)
    col_west = pltpu.roll(fields, cols - 1, 2)
    level_below = jnp.where(level == 0, fields, pltpu.roll(fields, 1, 1))
    level_above = jnp.where(level == lev - 1, fields, pltpu.roll(fields, lev - 1, 1))
    horizontal = row_north + row_south + col_east + col_west - 4.0 * fields
    new = fields + diff * horizontal + VERTICAL * (level_below + level_above - 2.0 * fields)
    if bounds is not None:
        row = r0 + lax.broadcasted_iota(jnp.int32, (count, 1, 1), 0)
        new = jnp.where((row >= bounds[0]) & (row < bounds[1]), new, 0.0)
    dst[pl.ds(out_r0, count)] = new


def _largest_divisor(n, limit):
    return max(k for k in range(1, limit + 1) if n % k == 0)


def _diffusion_kernel(bounds_ref, p_ref, o_ref, buf_a, buf_b):
    total = p_ref.shape[0]
    rows, lev = o_ref.shape[0], o_ref.shape[1]
    halo = (total - rows) // 2
    bounds = (bounds_ref[0], bounds_ref[1])
    chunk = _largest_divisor(total - 2, 16)
    src = p_ref
    targets = (buf_a, buf_b)
    for step in range(NSTEPS - 1):
        dst = targets[step % 2]
        dst[0] = src[0, pl.ds(0, lev)]
        dst[total - 1] = src[total - 1, pl.ds(0, lev)]

        def one(i, carry, src=src, dst=dst):
            r0 = 1 + i * chunk
            _advance_rows(src, dst, p_ref, r0, chunk, r0, bounds)
            return carry

        lax.fori_loop(0, (total - 2) // chunk, one, 0)
        src = dst
    last = _largest_divisor(rows, 16)

    def final(i, carry):
        _advance_rows(src, o_ref, p_ref, halo + i * last, last, i * last, None)
        return carry

    lax.fori_loop(0, rows // last, final, 0)


def diffuse(layer_temp, diffusivity):
    n_bands = lax.axis_size("band")
    band = lax.axis_index("band")
    rows = layer_temp.shape[1]
    lev = layer_temp.shape[2]
    cols = layer_temp.shape[3]
    halo = NSTEPS
    total = rows + 2 * halo
    comb = jnp.concatenate([layer_temp[0], diffusivity[0][:, None, :]], axis=1)
    forward = [(i, i + 1) for i in range(n_bands - 1)]
    backward = [(i + 1, i) for i in range(n_bands - 1)]
    above = lax.ppermute(comb[rows - halo:], "band", forward)
    below = lax.ppermute(comb[:halo], "band", backward)
    padded = jnp.concatenate([above, comb, below], axis=0)
    first = jnp.where(band == 0, halo, 0)
    stop = jnp.where(band == n_bands - 1, halo + rows, total)
    bounds = jnp.stack([first, stop]).astype(jnp.int32)
    return pl.pallas_call(
        _diffusion_kernel,
        out_shape=jax.ShapeDtypeStruct((rows, lev, cols), jnp.float32),
        in_specs=[
            pl.BlockSpec(memory_space=pltpu.SMEM),
            pl.BlockSpec(memory_space=pltpu.VMEM),
        ],
        out_specs=pl.BlockSpec(memory_space=pltpu.VMEM),
        scratch_shapes=[pltpu.VMEM((total, lev, cols), jnp.float32)] * 2,
    )(bounds, padded)


def body(layer_temp, diffusivity, owner_band, block_index, remap_blocks):
    n_sections = lax.axis_size("comp")
    n_bands = lax.axis_size("band")
    section = lax.axis_index("comp")
    rows = layer_temp.shape[1]
    cols = layer_temp.shape[3]
    width = NF * cols
    is_ocean = section == n_sections - 1
    weights_local = remap_blocks[0]

    surface_layers = layer_temp[0, :, :NF, :].astype(jnp.bfloat16)
    flux = lax.cond(
        is_ocean,
        lambda: jnp.zeros((rows, NF, cols), jnp.float32),
        lambda: jnp.einsum(
            "rfc,rcd->rfd", surface_layers, weights_local, preferred_element_type=jnp.float32
        ),
    )

    destination = owner_band[0, :, 0]
    dest_onehot = (destination[:, None] == jnp.arange(n_bands, dtype=jnp.int32)[None, :]).astype(
        jnp.float32
    )
    positions = jnp.arange(rows, dtype=jnp.int32)
    earlier_mask = (positions[:, None] > positions[None, :]).astype(jnp.float32)
    earlier = jnp.dot(
        earlier_mask.astype(jnp.bfloat16),
        dest_onehot.astype(jnp.bfloat16),
        preferred_element_type=jnp.float32,
    )
    slot_rank = jnp.sum(earlier * dest_onehot, axis=1).astype(jnp.int32)
    slot_onehot = (slot_rank[:, None] == jnp.arange(CAP, dtype=jnp.int32)[None, :]).astype(
        jnp.float32
    )
    selector = (dest_onehot[:, :, None] * slot_onehot[:, None, :]).reshape(rows, n_bands * CAP)

    index_lanes = jnp.broadcast_to(block_index[0].astype(jnp.float32)[:, None], (rows, 128))
    payload = jnp.concatenate([flux.reshape(rows, width), index_lanes], axis=1)
    sending = jnp.einsum("rk,rx->kx", selector, payload, precision=HIGHEST)
    sending = sending.reshape(n_bands, CAP, width + 128).astype(LINK)
    received = lax.all_to_all(sending, "band", 0, 0, tiled=True)
    received = received.reshape(n_bands * CAP, width + 128).astype(jnp.float32)
    got_index = received[:, width].astype(jnp.int32)
    match = (got_index[:, None] == positions[None, :]).astype(jnp.float32)
    partial = jnp.einsum("kr,kx->rx", match, received[:, :width], precision=HIGHEST)
    last = n_sections - 1
    part = COUPLING * partial
    if n_sections == 4:
        half = rows // 2
        up = lax.ppermute(part[:half].astype(LINK), "comp", [(1, 2)])
        down = lax.ppermute(part[half:].astype(LINK), "comp", [(1, 0)])
        carried = jnp.concatenate([up, down], axis=0).astype(jnp.float32)
        merged = (part + carried).astype(LINK)
        heating = lax.ppermute(merged, "comp", [(2, last)]).astype(jnp.float32)
        heating = heating + lax.ppermute(merged, "comp", [(0, last)]).astype(jnp.float32)
    else:
        scaled = part.astype(LINK)
        heating = scaled.astype(jnp.float32)
        for source in range(last):
            heating = heating + lax.ppermute(scaled, "comp", [(source, last)]).astype(
                jnp.float32
            )

    fields = diffuse(layer_temp, diffusivity)
    heating = jnp.where(is_ocean, heating, 0.0).reshape(rows, NF, cols)
    temp_out = fields.at[:, :NF].add(heating)
    sea_surface = temp_out[:, :NF].astype(jnp.bfloat16)
    returned = lax.cond(
        is_ocean,
        lambda: jnp.einsum(
            "rfc,rcd->rfd", sea_surface, weights_local, preferred_element_type=jnp.float32
        ).astype(jnp.bfloat16),
        lambda: jnp.zeros((rows, NF, cols), jnp.bfloat16),
    )

    ocean_rows = returned
    for target in range(last):
        ocean_rows = ocean_rows + lax.ppermute(returned, "comp", [(last, target)])
    ocean_rows = ocean_rows.reshape(rows, width)
    reply = jnp.einsum(
        "kr,rx->kx", match.astype(jnp.bfloat16), ocean_rows, preferred_element_type=jnp.float32
    ).astype(jnp.bfloat16)
    reply = reply.reshape(n_bands, CAP, width)
    came_back = lax.all_to_all(reply, "band", 0, 0, tiled=True)
    came_back = came_back.reshape(n_bands * CAP, width)
    seen = jnp.einsum(
        "rk,kx->rx", selector.astype(jnp.bfloat16), came_back, preferred_element_type=jnp.float32
    ).astype(jnp.bfloat16)
    surface_temp = jnp.where(is_ocean, returned, seen.reshape(rows, NF, cols))
    return temp_out[None], surface_temp[None]


def solution(mesh):
    return jax.shard_map(
        body,
        mesh=mesh,
        in_specs=(
            P("comp", "band", None, None),
            P("comp", "band", None),
            P("comp", "band", None),
            P("comp", "band"),
            P("comp", "band", None, None),
        ),
        out_specs=(P("comp", "band", None, None), P("comp", "band", None, None)),
        check_vma=False,
    )
```

```python
import jax
import jax.numpy as jnp
from jax import lax
from jax.sharding import PartitionSpec as P
from jax.experimental import pallas as pl
from jax.experimental.pallas import tpu as pltpu

NF = 4
NSTEPS = 4
CAP = 4

COUPLING = 0.25
VERTICAL = 0.15
HIGHEST = lax.Precision.HIGHEST
LINK = jnp.float16


def _advance_rows(src, dst, d_ref, r0, count, out_r0, bounds):
    lev, cols = dst.shape[1], dst.shape[2]
    fields = src[pl.ds(r0, count), pl.ds(0, lev)]
    row_north = src[pl.ds(r0 - 1, count), pl.ds(0, lev)]
    row_south = src[pl.ds(r0 + 1, count), pl.ds(0, lev)]
    diff = d_ref[pl.ds(r0, count), pl.ds(lev, 1)]
    level = lax.broadcasted_iota(jnp.int32, (count, lev, cols), 1)
    col_east = pltpu.roll(fields, 1, 2)
    col_west = pltpu.roll(fields, cols - 1, 2)
    level_below = jnp.where(level == 0, fields, pltpu.roll(fields, 1, 1))
    level_above = jnp.where(level == lev - 1, fields, pltpu.roll(fields, lev - 1, 1))
    horizontal = row_north + row_south + col_east + col_west - 4.0 * fields
    new = fields + diff * horizontal + VERTICAL * (level_below + level_above - 2.0 * fields)
    if bounds is not None:
        row = r0 + lax.broadcasted_iota(jnp.int32, (count, 1, 1), 0)
        new = jnp.where((row >= bounds[0]) & (row < bounds[1]), new, 0.0)
    dst[pl.ds(out_r0, count)] = new


def _largest_divisor(n, limit):
    return max(k for k in range(1, limit + 1) if n % k == 0)


def _diffusion_kernel(bounds_ref, p_ref, o_ref, buf_a, buf_b):
    total = p_ref.shape[0]
    rows, lev = o_ref.shape[0], o_ref.shape[1]
    halo = (total - rows) // 2
    bounds = (bounds_ref[0], bounds_ref[1])
    chunk = _largest_divisor(total - 2, 16)
    src = p_ref
    targets = (buf_a, buf_b)
    for step in range(NSTEPS - 1):
        dst = targets[step % 2]
        dst[0] = src[0, pl.ds(0, lev)]
        dst[total - 1] = src[total - 1, pl.ds(0, lev)]

        def one(i, carry, src=src, dst=dst):
            r0 = 1 + i * chunk
            _advance_rows(src, dst, p_ref, r0, chunk, r0, bounds)
            return carry

        lax.fori_loop(0, (total - 2) // chunk, one, 0)
        src = dst
    last = _largest_divisor(rows, 16)

    def final(i, carry):
        _advance_rows(src, o_ref, p_ref, halo + i * last, last, i * last, None)
        return carry

    lax.fori_loop(0, rows // last, final, 0)


def diffuse(layer_temp, diffusivity):
    n_bands = lax.axis_size("band")
    band = lax.axis_index("band")
    rows = layer_temp.shape[1]
    lev = layer_temp.shape[2]
    cols = layer_temp.shape[3]
    halo = NSTEPS
    total = rows + 2 * halo
    comb = jnp.concatenate([layer_temp[0], diffusivity[0][:, None, :]], axis=1)
    forward = [(i, i + 1) for i in range(n_bands - 1)]
    backward = [(i + 1, i) for i in range(n_bands - 1)]
    above = lax.ppermute(comb[rows - halo:], "band", forward)
    below = lax.ppermute(comb[:halo], "band", backward)
    padded = jnp.concatenate([above, comb, below], axis=0)
    first = jnp.where(band == 0, halo, 0)
    stop = jnp.where(band == n_bands - 1, halo + rows, total)
    bounds = jnp.stack([first, stop]).astype(jnp.int32)
    return pl.pallas_call(
        _diffusion_kernel,
        out_shape=jax.ShapeDtypeStruct((rows, lev, cols), jnp.float32),
        in_specs=[
            pl.BlockSpec(memory_space=pltpu.SMEM),
            pl.BlockSpec(memory_space=pltpu.VMEM),
        ],
        out_specs=pl.BlockSpec(memory_space=pltpu.VMEM),
        scratch_shapes=[pltpu.VMEM((total, lev, cols), jnp.float32)] * 2,
    )(bounds, padded)


def body(layer_temp, diffusivity, owner_band, block_index, remap_blocks):
    n_sections = lax.axis_size("comp")
    n_bands = lax.axis_size("band")
    section = lax.axis_index("comp")
    rows = layer_temp.shape[1]
    cols = layer_temp.shape[3]
    width = NF * cols
    is_ocean = section == n_sections - 1
    weights_local = remap_blocks[0]

    surface_layers = layer_temp[0, :, :NF, :].astype(jnp.bfloat16)
    flux = lax.cond(
        is_ocean,
        lambda: jnp.zeros((rows, NF, cols), jnp.float32),
        lambda: jnp.einsum(
            "rfc,rcd->rfd", surface_layers, weights_local, preferred_element_type=jnp.float32
        ),
    )

    destination = owner_band[0, :, 0]
    dest_onehot = (destination[:, None] == jnp.arange(n_bands, dtype=jnp.int32)[None, :]).astype(
        jnp.float32
    )
    positions = jnp.arange(rows, dtype=jnp.int32)
    earlier_mask = (positions[:, None] > positions[None, :]).astype(jnp.float32)
    earlier = jnp.dot(
        earlier_mask.astype(jnp.bfloat16),
        dest_onehot.astype(jnp.bfloat16),
        preferred_element_type=jnp.float32,
    )
    slot_rank = jnp.sum(earlier * dest_onehot, axis=1).astype(jnp.int32)
    slot_onehot = (slot_rank[:, None] == jnp.arange(CAP, dtype=jnp.int32)[None, :]).astype(
        jnp.float32
    )
    selector = (dest_onehot[:, :, None] * slot_onehot[:, None, :]).reshape(rows, n_bands * CAP)

    index_lanes = jnp.broadcast_to(block_index[0].astype(jnp.float32)[:, None], (rows, 128))
    payload = jnp.concatenate([flux.reshape(rows, width), index_lanes], axis=1)
    sending = jnp.einsum("rk,rx->kx", selector, payload, precision=HIGHEST)
    sending = sending.reshape(n_bands, CAP, width + 128).astype(LINK)
    received = lax.all_to_all(sending, "band", 0, 0, tiled=True)
    received = received.reshape(n_bands * CAP, width + 128).astype(jnp.float32)
    got_index = received[:, width].astype(jnp.int32)
    match = (got_index[:, None] == positions[None, :]).astype(jnp.float32)
    partial = jnp.einsum("kr,kx->rx", match, received[:, :width], precision=HIGHEST)
    last = n_sections - 1
    scaled = (COUPLING * partial).astype(LINK)
    heating = scaled.astype(jnp.float32)
    for source in range(last):
        heating = heating + lax.ppermute(scaled, "comp", [(source, last)]).astype(jnp.float32)

    fields = diffuse(layer_temp, diffusivity)
    heating = jnp.where(is_ocean, heating, 0.0).reshape(rows, NF, cols)
    temp_out = fields.at[:, :NF].add(heating)
    returned = lax.cond(
        is_ocean,
        lambda: jnp.einsum(
            "rfc,rcd->rfd",
            (fields[:, :NF] + heating).astype(jnp.bfloat16),
            weights_local,
            preferred_element_type=jnp.float32,
        ).astype(jnp.bfloat16),
        lambda: jnp.zeros((rows, NF, cols), jnp.bfloat16),
    )

    ocean_rows = returned
    for target in range(last):
        ocean_rows = ocean_rows + lax.ppermute(returned, "comp", [(last, target)])
    ocean_rows = ocean_rows.reshape(rows, width)
    reply = jnp.einsum(
        "kr,rx->kx", match.astype(jnp.bfloat16), ocean_rows, preferred_element_type=jnp.float32
    ).astype(jnp.bfloat16)
    reply = reply.reshape(n_bands, CAP, width)
    came_back = lax.all_to_all(reply, "band", 0, 0, tiled=True)
    came_back = came_back.reshape(n_bands * CAP, width)
    seen = jnp.einsum(
        "rk,kx->rx", selector.astype(jnp.bfloat16), came_back, preferred_element_type=jnp.float32
    ).astype(jnp.bfloat16)
    surface_temp = jnp.where(is_ocean, returned, seen.reshape(rows, NF, cols))
    return temp_out[None], surface_temp[None]


def solution(mesh):
    return jax.shard_map(
        body,
        mesh=mesh,
        in_specs=(
            P("comp", "band", None, None),
            P("comp", "band", None),
            P("comp", "band", None),
            P("comp", "band"),
            P("comp", "band", None, None),
        ),
        out_specs=(P("comp", "band", None, None), P("comp", "band", None, None)),
        check_vma=False,
    )
```

```python
import jax
import jax.numpy as jnp
from jax import lax
from jax.sharding import PartitionSpec as P
from jax.experimental import pallas as pl
from jax.experimental.pallas import tpu as pltpu

NF = 4
NSTEPS = 4
CAP = 4

COUPLING = 0.25
VERTICAL = 0.15
HIGHEST = lax.Precision.HIGHEST
LINK = jnp.float16


def _advance_rows(src, dst, d_ref, r0, count, out_r0, bounds):
    lev, cols = dst.shape[1], dst.shape[2]
    fields = src[pl.ds(r0, count), pl.ds(0, lev)]
    row_north = src[pl.ds(r0 - 1, count), pl.ds(0, lev)]
    row_south = src[pl.ds(r0 + 1, count), pl.ds(0, lev)]
    diff = d_ref[pl.ds(r0, count), pl.ds(lev, 1)]
    level = lax.broadcasted_iota(jnp.int32, (count, lev, cols), 1)
    col_east = pltpu.roll(fields, 1, 2)
    col_west = pltpu.roll(fields, cols - 1, 2)
    level_below = jnp.where(level == 0, fields, pltpu.roll(fields, 1, 1))
    level_above = jnp.where(level == lev - 1, fields, pltpu.roll(fields, lev - 1, 1))
    horizontal = row_north + row_south + col_east + col_west - 4.0 * fields
    new = fields + diff * horizontal + VERTICAL * (level_below + level_above - 2.0 * fields)
    if bounds is not None:
        row = r0 + lax.broadcasted_iota(jnp.int32, (count, 1, 1), 0)
        new = jnp.where((row >= bounds[0]) & (row < bounds[1]), new, 0.0)
    dst[pl.ds(out_r0, count)] = new


def _largest_divisor(n, limit):
    return max(k for k in range(1, limit + 1) if n % k == 0)


def _diffusion_kernel(bounds_ref, p_ref, o_ref, buf_a, buf_b):
    total = p_ref.shape[0]
    rows, lev = o_ref.shape[0], o_ref.shape[1]
    halo = (total - rows) // 2
    bounds = (bounds_ref[0], bounds_ref[1])
    chunk = _largest_divisor(total - 2, 16)
    src = p_ref
    targets = (buf_a, buf_b)
    for step in range(NSTEPS - 1):
        dst = targets[step % 2]
        dst[0] = src[0, pl.ds(0, lev)]
        dst[total - 1] = src[total - 1, pl.ds(0, lev)]

        def one(i, carry, src=src, dst=dst):
            r0 = 1 + i * chunk
            _advance_rows(src, dst, p_ref, r0, chunk, r0, bounds)
            return carry

        lax.fori_loop(0, (total - 2) // chunk, one, 0)
        src = dst
    last = _largest_divisor(rows, 16)

    def final(i, carry):
        _advance_rows(src, o_ref, p_ref, halo + i * last, last, i * last, None)
        return carry

    lax.fori_loop(0, rows // last, final, 0)


def diffuse(layer_temp, diffusivity):
    n_bands = lax.axis_size("band")
    band = lax.axis_index("band")
    rows = layer_temp.shape[1]
    lev = layer_temp.shape[2]
    cols = layer_temp.shape[3]
    halo = NSTEPS
    total = rows + 2 * halo
    comb = jnp.concatenate([layer_temp[0], diffusivity[0][:, None, :]], axis=1)
    forward = [(i, i + 1) for i in range(n_bands - 1)]
    backward = [(i + 1, i) for i in range(n_bands - 1)]
    above = lax.ppermute(comb[rows - halo:], "band", forward)
    below = lax.ppermute(comb[:halo], "band", backward)
    padded = jnp.concatenate([above, comb, below], axis=0)
    first = jnp.where(band == 0, halo, 0)
    stop = jnp.where(band == n_bands - 1, halo + rows, total)
    bounds = jnp.stack([first, stop]).astype(jnp.int32)
    return pl.pallas_call(
        _diffusion_kernel,
        out_shape=jax.ShapeDtypeStruct((rows, lev, cols), jnp.float32),
        in_specs=[
            pl.BlockSpec(memory_space=pltpu.SMEM),
            pl.BlockSpec(memory_space=pltpu.VMEM),
        ],
        out_specs=pl.BlockSpec(memory_space=pltpu.VMEM),
        scratch_shapes=[pltpu.VMEM((total, lev, cols), jnp.float32)] * 2,
    )(bounds, padded)


def body(layer_temp, diffusivity, owner_band, block_index, remap_blocks):
    n_sections = lax.axis_size("comp")
    n_bands = lax.axis_size("band")
    section = lax.axis_index("comp")
    rows = layer_temp.shape[1]
    cols = layer_temp.shape[3]
    width = NF * cols
    is_ocean = section == n_sections - 1
    weights_local = remap_blocks[0]

    surface_layers = layer_temp[0, :, :NF, :].astype(jnp.bfloat16)
    flux = lax.cond(
        is_ocean,
        lambda: jnp.zeros((rows, NF, cols), jnp.float32),
        lambda: jnp.einsum(
            "rfc,rcd->rfd", surface_layers, weights_local, preferred_element_type=jnp.float32
        ),
    )

    destination = owner_band[0, :, 0]
    dest_onehot = (destination[:, None] == jnp.arange(n_bands, dtype=jnp.int32)[None, :]).astype(
        jnp.float32
    )
    positions = jnp.arange(rows, dtype=jnp.int32)
    earlier_mask = (positions[:, None] > positions[None, :]).astype(jnp.float32)
    earlier = jnp.dot(
        earlier_mask.astype(jnp.bfloat16),
        dest_onehot.astype(jnp.bfloat16),
        preferred_element_type=jnp.float32,
    )
    slot_rank = jnp.sum(earlier * dest_onehot, axis=1).astype(jnp.int32)
    slot_onehot = (slot_rank[:, None] == jnp.arange(CAP, dtype=jnp.int32)[None, :]).astype(
        jnp.float32
    )
    selector = (dest_onehot[:, :, None] * slot_onehot[:, None, :]).reshape(rows, n_bands * CAP)

    index_lanes = jnp.broadcast_to(block_index[0].astype(jnp.float32)[:, None], (rows, 128))
    payload = jnp.concatenate([flux.reshape(rows, width), index_lanes], axis=1)
    sending = jnp.einsum("rk,rx->kx", selector, payload, precision=HIGHEST)
    sending = sending.reshape(n_bands, CAP, width + 128).astype(LINK)
    received = lax.all_to_all(sending, "band", 0, 0, tiled=True)
    received = received.reshape(n_bands * CAP, width + 128).astype(jnp.float32)
    got_index = received[:, width].astype(jnp.int32)
    match = (got_index[:, None] == positions[None, :]).astype(jnp.float32)
    partial = jnp.einsum("kr,kx->rx", match, received[:, :width], precision=HIGHEST)
    last = n_sections - 1
    scaled = (COUPLING * partial).astype(LINK)
    heating = scaled.astype(jnp.float32)
    for source in range(last):
        heating = heating + lax.ppermute(scaled, "comp", [(source, last)]).astype(jnp.float32)

    fields = diffuse(layer_temp, diffusivity)
    heating = jnp.where(is_ocean, heating, 0.0).reshape(rows, NF, cols)
    temp_out = fields.at[:, :NF].add(heating)
    returned = lax.cond(
        is_ocean,
        lambda: jnp.einsum(
            "rfc,rcd->rfd",
            (fields[:, :NF] + heating).astype(jnp.bfloat16),
            weights_local,
            preferred_element_type=jnp.float32,
        ).astype(jnp.bfloat16),
        lambda: jnp.zeros((rows, NF, cols), jnp.bfloat16),
    )

    ocean_rows = returned
    for target in range(last):
        ocean_rows = ocean_rows + lax.ppermute(returned, "comp", [(last, target)])
    ocean_rows = ocean_rows.reshape(rows, width)
    reply = jnp.take(ocean_rows, got_index.reshape(n_bands, CAP), axis=0)
    came_back = lax.all_to_all(reply, "band", 0, 0, tiled=True)
    came_back = came_back.reshape(n_bands, CAP, NF, cols)
    seen = came_back[destination, slot_rank]
    surface_temp = jnp.where(is_ocean, returned, seen)
    return temp_out[None], surface_temp[None]


def solution(mesh):
    return jax.shard_map(
        body,
        mesh=mesh,
        in_specs=(
            P("comp", "band", None, None),
            P("comp", "band", None),
            P("comp", "band", None),
            P("comp", "band"),
            P("comp", "band", None, None),
        ),
        out_specs=(P("comp", "band", None, None), P("comp", "band", None, None)),
        check_vma=False,
    )
```

```python
import jax
import jax.numpy as jnp
from jax import lax
from jax.sharding import PartitionSpec as P
from jax.experimental import pallas as pl
from jax.experimental.pallas import tpu as pltpu

NF = 4
NSTEPS = 4
CAP = 4

COUPLING = 0.25
VERTICAL = 0.15
HIGHEST = lax.Precision.HIGHEST
LINK = jnp.float16


def _advance_rows(src, dst, d_ref, r0, count, out_r0, bounds):
    lev, cols = dst.shape[1], dst.shape[2]
    fields = src[pl.ds(r0, count), pl.ds(0, lev)]
    row_north = src[pl.ds(r0 - 1, count), pl.ds(0, lev)]
    row_south = src[pl.ds(r0 + 1, count), pl.ds(0, lev)]
    diff = d_ref[pl.ds(r0, count), pl.ds(lev, 1)]
    level = lax.broadcasted_iota(jnp.int32, (count, lev, cols), 1)
    col_east = pltpu.roll(fields, 1, 2)
    col_west = pltpu.roll(fields, cols - 1, 2)
    level_below = jnp.where(level == 0, fields, pltpu.roll(fields, 1, 1))
    level_above = jnp.where(level == lev - 1, fields, pltpu.roll(fields, lev - 1, 1))
    horizontal = row_north + row_south + col_east + col_west - 4.0 * fields
    new = fields + diff * horizontal + VERTICAL * (level_below + level_above - 2.0 * fields)
    if bounds is not None:
        row = r0 + lax.broadcasted_iota(jnp.int32, (count, 1, 1), 0)
        new = jnp.where((row >= bounds[0]) & (row < bounds[1]), new, 0.0)
    dst[pl.ds(out_r0, count)] = new


def _largest_divisor(n, limit):
    return max(k for k in range(1, limit + 1) if n % k == 0)


def _diffusion_kernel(bounds_ref, p_ref, o_ref, buf_a, buf_b):
    total = p_ref.shape[0]
    rows, lev = o_ref.shape[0], o_ref.shape[1]
    halo = (total - rows) // 2
    bounds = (bounds_ref[0], bounds_ref[1])
    chunk = _largest_divisor(total - 2, 16)
    src = p_ref
    targets = (buf_a, buf_b)
    for step in range(NSTEPS - 1):
        dst = targets[step % 2]
        dst[0] = src[0, pl.ds(0, lev)]
        dst[total - 1] = src[total - 1, pl.ds(0, lev)]

        def one(i, carry, src=src, dst=dst):
            r0 = 1 + i * chunk
            _advance_rows(src, dst, p_ref, r0, chunk, r0, bounds)
            return carry

        lax.fori_loop(0, (total - 2) // chunk, one, 0)
        src = dst
    last = _largest_divisor(rows, 16)

    def final(i, carry):
        _advance_rows(src, o_ref, p_ref, halo + i * last, last, i * last, None)
        return carry

    lax.fori_loop(0, rows // last, final, 0)


def diffuse(layer_temp, diffusivity):
    n_bands = lax.axis_size("band")
    band = lax.axis_index("band")
    rows = layer_temp.shape[1]
    lev = layer_temp.shape[2]
    cols = layer_temp.shape[3]
    halo = NSTEPS
    total = rows + 2 * halo
    comb = jnp.concatenate([layer_temp[0], diffusivity[0][:, None, :]], axis=1)
    forward = [(i, i + 1) for i in range(n_bands - 1)]
    backward = [(i + 1, i) for i in range(n_bands - 1)]
    above = lax.ppermute(comb[rows - halo:], "band", forward)
    below = lax.ppermute(comb[:halo], "band", backward)
    padded = jnp.concatenate([above, comb, below], axis=0)
    first = jnp.where(band == 0, halo, 0)
    stop = jnp.where(band == n_bands - 1, halo + rows, total)
    bounds = jnp.stack([first, stop]).astype(jnp.int32)
    return pl.pallas_call(
        _diffusion_kernel,
        out_shape=jax.ShapeDtypeStruct((rows, lev, cols), jnp.float32),
        in_specs=[
            pl.BlockSpec(memory_space=pltpu.SMEM),
            pl.BlockSpec(memory_space=pltpu.VMEM),
        ],
        out_specs=pl.BlockSpec(memory_space=pltpu.VMEM),
        scratch_shapes=[pltpu.VMEM((total, lev, cols), jnp.float32)] * 2,
    )(bounds, padded)


def body(layer_temp, diffusivity, owner_band, block_index, remap_blocks):
    n_sections = lax.axis_size("comp")
    n_bands = lax.axis_size("band")
    section = lax.axis_index("comp")
    rows = layer_temp.shape[1]
    cols = layer_temp.shape[3]
    width = NF * cols
    is_ocean = section == n_sections - 1
    weights_local = remap_blocks[0]

    surface_layers = layer_temp[0, :, :NF, :].astype(jnp.bfloat16)
    flux = lax.cond(
        is_ocean,
        lambda: jnp.zeros((rows, NF, cols), jnp.float32),
        lambda: jnp.einsum(
            "rfc,rcd->rfd", surface_layers, weights_local, preferred_element_type=jnp.float32
        ),
    )

    destination = owner_band[0, :, 0]
    dest_onehot = (destination[:, None] == jnp.arange(n_bands, dtype=jnp.int32)[None, :]).astype(
        jnp.float32
    )
    positions = jnp.arange(rows, dtype=jnp.int32)
    earlier_mask = (positions[:, None] > positions[None, :]).astype(jnp.float32)
    earlier = jnp.dot(
        earlier_mask.astype(jnp.bfloat16),
        dest_onehot.astype(jnp.bfloat16),
        preferred_element_type=jnp.float32,
    )
    slot_rank = jnp.sum(earlier * dest_onehot, axis=1).astype(jnp.int32)
    slot_onehot = (slot_rank[:, None] == jnp.arange(CAP, dtype=jnp.int32)[None, :]).astype(
        jnp.float32
    )
    selector = (dest_onehot[:, :, None] * slot_onehot[:, None, :]).reshape(rows, n_bands * CAP)

    index_lanes = jnp.broadcast_to(block_index[0].astype(jnp.float32)[:, None], (rows, 128))
    payload = jnp.concatenate([flux.reshape(rows, width), index_lanes], axis=1)
    sending = jnp.einsum("rk,rx->kx", selector, payload, precision=HIGHEST)
    sending = sending.reshape(n_bands, CAP, width + 128).astype(LINK)
    received = lax.all_to_all(sending, "band", 0, 0, tiled=True)
    received = received.reshape(n_bands * CAP, width + 128).astype(jnp.float32)
    got_index = received[:, width].astype(jnp.int32)
    match = (got_index[:, None] == positions[None, :]).astype(jnp.float32)
    partial = jnp.einsum("kr,kx->rx", match, received[:, :width], precision=HIGHEST)
    last = n_sections - 1
    scaled = (COUPLING * partial).astype(LINK)
    heating = scaled.astype(jnp.float32)
    for source in sorted(range(last), key=lambda t: (t + 1) % last):
        heating = heating + lax.ppermute(scaled, "comp", [(source, last)]).astype(jnp.float32)

    fields = diffuse(layer_temp, diffusivity)
    heating = jnp.where(is_ocean, heating, 0.0).reshape(rows, NF, cols)
    temp_out = fields.at[:, :NF].add(heating)
    returned = lax.cond(
        is_ocean,
        lambda: jnp.einsum(
            "rfc,rcd->rfd",
            (fields[:, :NF] + heating).astype(jnp.bfloat16),
            weights_local,
            preferred_element_type=jnp.float32,
        ).astype(jnp.bfloat16),
        lambda: jnp.zeros((rows, NF, cols), jnp.bfloat16),
    )

    ocean_rows = returned
    for target in range(last):
        ocean_rows = ocean_rows + lax.ppermute(returned, "comp", [(last, target)])
    ocean_rows = ocean_rows.reshape(rows, width)
    reply = jnp.einsum(
        "kr,rx->kx", match.astype(jnp.bfloat16), ocean_rows, preferred_element_type=jnp.float32
    ).astype(jnp.bfloat16)
    reply = reply.reshape(n_bands, CAP, width)
    came_back = lax.all_to_all(reply, "band", 0, 0, tiled=True)
    came_back = came_back.reshape(n_bands * CAP, width)
    seen = jnp.einsum(
        "rk,kx->rx", selector.astype(jnp.bfloat16), came_back, preferred_element_type=jnp.float32
    ).astype(jnp.bfloat16)
    surface_temp = jnp.where(is_ocean, returned, seen.reshape(rows, NF, cols))
    return temp_out[None], surface_temp[None]


def solution(mesh):
    return jax.shard_map(
        body,
        mesh=mesh,
        in_specs=(
            P("comp", "band", None, None),
            P("comp", "band", None),
            P("comp", "band", None),
            P("comp", "band"),
            P("comp", "band", None, None),
        ),
        out_specs=(P("comp", "band", None, None), P("comp", "band", None, None)),
        check_vma=False,
    )
```

```python
import jax
import jax.numpy as jnp
from jax import lax
from jax.sharding import PartitionSpec as P
from jax.experimental import pallas as pl
from jax.experimental.pallas import tpu as pltpu

NF = 4
NSTEPS = 4
CAP = 4

COUPLING = 0.25
VERTICAL = 0.15
HIGHEST = lax.Precision.HIGHEST
LINK = jnp.float16


def _advance_rows(src, dst, d_ref, r0, count, out_r0, bounds):
    lev, cols = dst.shape[1], dst.shape[2]
    fields = src[pl.ds(r0, count), pl.ds(0, lev)]
    row_north = src[pl.ds(r0 - 1, count), pl.ds(0, lev)]
    row_south = src[pl.ds(r0 + 1, count), pl.ds(0, lev)]
    diff = d_ref[pl.ds(r0, count), pl.ds(lev, 1)]
    level = lax.broadcasted_iota(jnp.int32, (count, lev, cols), 1)
    col_east = pltpu.roll(fields, 1, 2)
    col_west = pltpu.roll(fields, cols - 1, 2)
    level_below = jnp.where(level == 0, fields, pltpu.roll(fields, 1, 1))
    level_above = jnp.where(level == lev - 1, fields, pltpu.roll(fields, lev - 1, 1))
    horizontal = row_north + row_south + col_east + col_west - 4.0 * fields
    new = fields + diff * horizontal + VERTICAL * (level_below + level_above - 2.0 * fields)
    if bounds is not None:
        row = r0 + lax.broadcasted_iota(jnp.int32, (count, 1, 1), 0)
        new = jnp.where((row >= bounds[0]) & (row < bounds[1]), new, 0.0)
    dst[pl.ds(out_r0, count)] = new


def _largest_divisor(n, limit):
    return max(k for k in range(1, limit + 1) if n % k == 0)


def _diffusion_kernel(bounds_ref, p_ref, o_ref, buf_a, buf_b):
    total = p_ref.shape[0]
    rows, lev = o_ref.shape[0], o_ref.shape[1]
    halo = (total - rows) // 2
    bounds = (bounds_ref[0], bounds_ref[1])
    chunk = _largest_divisor(total - 2, 16)
    src = p_ref
    targets = (buf_a, buf_b)
    for step in range(NSTEPS - 1):
        dst = targets[step % 2]
        dst[0] = src[0, pl.ds(0, lev)]
        dst[total - 1] = src[total - 1, pl.ds(0, lev)]

        def one(i, carry, src=src, dst=dst):
            r0 = 1 + i * chunk
            _advance_rows(src, dst, p_ref, r0, chunk, r0, bounds)
            return carry

        lax.fori_loop(0, (total - 2) // chunk, one, 0)
        src = dst
    last = _largest_divisor(rows, 16)

    def final(i, carry):
        _advance_rows(src, o_ref, p_ref, halo + i * last, last, i * last, None)
        return carry

    lax.fori_loop(0, rows // last, final, 0)


def diffuse(layer_temp, diffusivity):
    n_bands = lax.axis_size("band")
    band = lax.axis_index("band")
    rows = layer_temp.shape[1]
    lev = layer_temp.shape[2]
    cols = layer_temp.shape[3]
    halo = NSTEPS
    total = rows + 2 * halo
    comb = jnp.concatenate([layer_temp[0], diffusivity[0][:, None, :]], axis=1)
    forward = [(i, i + 1) for i in range(n_bands - 1)]
    backward = [(i + 1, i) for i in range(n_bands - 1)]
    above = lax.ppermute(comb[rows - halo:], "band", forward)
    below = lax.ppermute(comb[:halo], "band", backward)
    padded = jnp.concatenate([above, comb, below], axis=0)
    first = jnp.where(band == 0, halo, 0)
    stop = jnp.where(band == n_bands - 1, halo + rows, total)
    bounds = jnp.stack([first, stop]).astype(jnp.int32)
    return pl.pallas_call(
        _diffusion_kernel,
        out_shape=jax.ShapeDtypeStruct((rows, lev, cols), jnp.float32),
        in_specs=[
            pl.BlockSpec(memory_space=pltpu.SMEM),
            pl.BlockSpec(memory_space=pltpu.VMEM),
        ],
        out_specs=pl.BlockSpec(memory_space=pltpu.VMEM),
        scratch_shapes=[pltpu.VMEM((total, lev, cols), jnp.float32)] * 2,
    )(bounds, padded)


def body(layer_temp, diffusivity, owner_band, block_index, remap_blocks):
    n_sections = lax.axis_size("comp")
    n_bands = lax.axis_size("band")
    section = lax.axis_index("comp")
    rows = layer_temp.shape[1]
    cols = layer_temp.shape[3]
    width = NF * cols
    is_ocean = section == n_sections - 1
    weights_local = remap_blocks[0]

    surface_layers = layer_temp[0, :, :NF, :].astype(jnp.bfloat16)
    flux = lax.cond(
        is_ocean,
        lambda: jnp.zeros((rows, NF, cols), jnp.float32),
        lambda: jnp.einsum(
            "rfc,rcd->rfd", surface_layers, weights_local, preferred_element_type=jnp.float32
        ),
    )

    destination = owner_band[0, :, 0]
    dest_onehot = (destination[:, None] == jnp.arange(n_bands, dtype=jnp.int32)[None, :]).astype(
        jnp.float32
    )
    positions = jnp.arange(rows, dtype=jnp.int32)
    earlier_mask = (positions[:, None] > positions[None, :]).astype(jnp.float32)
    earlier = jnp.dot(
        earlier_mask.astype(jnp.bfloat16),
        dest_onehot.astype(jnp.bfloat16),
        preferred_element_type=jnp.float32,
    )
    slot_rank = jnp.sum(earlier * dest_onehot, axis=1).astype(jnp.int32)
    slot_onehot = (slot_rank[:, None] == jnp.arange(CAP, dtype=jnp.int32)[None, :]).astype(
        jnp.float32
    )
    selector = (dest_onehot[:, :, None] * slot_onehot[:, None, :]).reshape(rows, n_bands * CAP)

    index_lanes = jnp.broadcast_to(block_index[0].astype(jnp.float32)[:, None], (rows, 128))
    payload = jnp.concatenate([flux.reshape(rows, width), index_lanes], axis=1)
    sending = jnp.einsum("rk,rx->kx", selector, payload, precision=HIGHEST)
    sending = sending.reshape(n_bands, CAP, width + 128).astype(LINK)
    received = lax.all_to_all(sending, "band", 0, 0, tiled=True)
    received = received.reshape(n_bands * CAP, width + 128).astype(jnp.float32)
    got_index = received[:, width].astype(jnp.int32)
    match = (got_index[:, None] == positions[None, :]).astype(jnp.float32)
    partial = jnp.einsum("kr,kx->rx", match, received[:, :width], precision=HIGHEST)
    last = n_sections - 1
    scaled = (COUPLING * partial).astype(LINK)
    heating = scaled.astype(jnp.float32)
    for source in sorted(range(last), key=lambda t: (t + 1) % last):
        heating = heating + lax.ppermute(scaled, "comp", [(source, last)]).astype(jnp.float32)

    fields = diffuse(layer_temp, diffusivity)
    heating = jnp.where(is_ocean, heating, 0.0).reshape(rows, NF, cols)
    temp_out = fields.at[:, :NF].add(heating)
    returned = lax.cond(
        is_ocean,
        lambda: jnp.einsum(
            "rfc,rcd->rfd",
            (fields[:, :NF] + heating).astype(jnp.bfloat16),
            weights_local,
            preferred_element_type=jnp.float32,
        ).astype(jnp.bfloat16),
        lambda: jnp.zeros((rows, NF, cols), jnp.bfloat16),
    )

    ocean_rows = returned
    for target in sorted(range(last), key=lambda t: (t + 1) % last):
        ocean_rows = ocean_rows + lax.ppermute(returned, "comp", [(last, target)])
    ocean_rows = ocean_rows.reshape(rows, width)
    reply = jnp.einsum(
        "kr,rx->kx", match.astype(jnp.bfloat16), ocean_rows, preferred_element_type=jnp.float32
    ).astype(jnp.bfloat16)
    reply = reply.reshape(n_bands, CAP, width)
    came_back = lax.all_to_all(reply, "band", 0, 0, tiled=True)
    came_back = came_back.reshape(n_bands * CAP, width)
    seen = jnp.einsum(
        "rk,kx->rx", selector.astype(jnp.bfloat16), came_back, preferred_element_type=jnp.float32
    ).astype(jnp.bfloat16)
    surface_temp = jnp.where(is_ocean, returned, seen.reshape(rows, NF, cols))
    return temp_out[None], surface_temp[None]


def solution(mesh):
    return jax.shard_map(
        body,
        mesh=mesh,
        in_specs=(
            P("comp", "band", None, None),
            P("comp", "band", None),
            P("comp", "band", None),
            P("comp", "band"),
            P("comp", "band", None, None),
        ),
        out_specs=(P("comp", "band", None, None), P("comp", "band", None, None)),
        check_vma=False,
    )
```

```python
import jax
import jax.numpy as jnp
from jax import lax
from jax.sharding import PartitionSpec as P
from jax.experimental import pallas as pl
from jax.experimental.pallas import tpu as pltpu

NF = 4
NSTEPS = 4
CAP = 4

COUPLING = 0.25
VERTICAL = 0.15
HIGHEST = lax.Precision.HIGHEST
LINK = jnp.float16


def _advance_rows(src, dst, d_ref, r0, count, out_r0, bounds):
    lev, cols = dst.shape[1], dst.shape[2]
    fields = src[pl.ds(r0, count), pl.ds(0, lev)]
    row_north = src[pl.ds(r0 - 1, count), pl.ds(0, lev)]
    row_south = src[pl.ds(r0 + 1, count), pl.ds(0, lev)]
    diff = d_ref[pl.ds(r0, count), pl.ds(lev, 1)]
    level = lax.broadcasted_iota(jnp.int32, (count, lev, cols), 1)
    col_east = pltpu.roll(fields, 1, 2)
    col_west = pltpu.roll(fields, cols - 1, 2)
    level_below = jnp.where(level == 0, fields, pltpu.roll(fields, 1, 1))
    level_above = jnp.where(level == lev - 1, fields, pltpu.roll(fields, lev - 1, 1))
    horizontal = row_north + row_south + col_east + col_west - 4.0 * fields
    new = fields + diff * horizontal + VERTICAL * (level_below + level_above - 2.0 * fields)
    if bounds is not None:
        row = r0 + lax.broadcasted_iota(jnp.int32, (count, 1, 1), 0)
        new = jnp.where((row >= bounds[0]) & (row < bounds[1]), new, 0.0)
    dst[pl.ds(out_r0, count)] = new


def _largest_divisor(n, limit):
    return max(k for k in range(1, limit + 1) if n % k == 0)


def _diffusion_kernel(bounds_ref, p_ref, o_ref, buf_a, buf_b):
    total = p_ref.shape[0]
    rows, lev = o_ref.shape[0], o_ref.shape[1]
    halo = (total - rows) // 2
    bounds = (bounds_ref[0], bounds_ref[1])
    chunk = _largest_divisor(total - 2, 16)
    src = p_ref
    targets = (buf_a, buf_b)
    for step in range(NSTEPS - 1):
        dst = targets[step % 2]
        dst[0] = src[0, pl.ds(0, lev)]
        dst[total - 1] = src[total - 1, pl.ds(0, lev)]

        def one(i, carry, src=src, dst=dst):
            r0 = 1 + i * chunk
            _advance_rows(src, dst, p_ref, r0, chunk, r0, bounds)
            return carry

        lax.fori_loop(0, (total - 2) // chunk, one, 0)
        src = dst
    last = _largest_divisor(rows, 16)

    def final(i, carry):
        _advance_rows(src, o_ref, p_ref, halo + i * last, last, i * last, None)
        return carry

    lax.fori_loop(0, rows // last, final, 0)


def diffuse(layer_temp, diffusivity):
    n_bands = lax.axis_size("band")
    band = lax.axis_index("band")
    rows = layer_temp.shape[1]
    lev = layer_temp.shape[2]
    cols = layer_temp.shape[3]
    halo = NSTEPS
    total = rows + 2 * halo
    comb = jnp.concatenate([layer_temp[0], diffusivity[0][:, None, :]], axis=1)
    forward = [(i, i + 1) for i in range(n_bands - 1)]
    backward = [(i + 1, i) for i in range(n_bands - 1)]
    above = lax.ppermute(comb[rows - halo:], "band", forward)
    below = lax.ppermute(comb[:halo], "band", backward)
    padded = jnp.concatenate([above, comb, below], axis=0)
    first = jnp.where(band == 0, halo, 0)
    stop = jnp.where(band == n_bands - 1, halo + rows, total)
    bounds = jnp.stack([first, stop]).astype(jnp.int32)
    return pl.pallas_call(
        _diffusion_kernel,
        out_shape=jax.ShapeDtypeStruct((rows, lev, cols), jnp.float32),
        in_specs=[
            pl.BlockSpec(memory_space=pltpu.SMEM),
            pl.BlockSpec(memory_space=pltpu.VMEM),
        ],
        out_specs=pl.BlockSpec(memory_space=pltpu.VMEM),
        scratch_shapes=[pltpu.VMEM((total, lev, cols), jnp.float32)] * 2,
    )(bounds, padded)


def body(layer_temp, diffusivity, owner_band, block_index, remap_blocks):
    n_sections = lax.axis_size("comp")
    n_bands = lax.axis_size("band")
    section = lax.axis_index("comp")
    rows = layer_temp.shape[1]
    cols = layer_temp.shape[3]
    width = NF * cols
    is_ocean = section == n_sections - 1
    weights_local = remap_blocks[0]

    surface_layers = layer_temp[0, :, :NF, :].astype(jnp.bfloat16)
    flux = lax.cond(
        is_ocean,
        lambda: jnp.zeros((rows, NF, cols), jnp.float32),
        lambda: jnp.einsum(
            "rfc,rcd->rfd", surface_layers, weights_local, preferred_element_type=jnp.float32
        ),
    )

    destination = owner_band[0, :, 0]
    dest_onehot = (destination[:, None] == jnp.arange(n_bands, dtype=jnp.int32)[None, :]).astype(
        jnp.float32
    )
    positions = jnp.arange(rows, dtype=jnp.int32)
    earlier_mask = (positions[:, None] > positions[None, :]).astype(jnp.float32)
    earlier = jnp.dot(
        earlier_mask.astype(jnp.bfloat16),
        dest_onehot.astype(jnp.bfloat16),
        preferred_element_type=jnp.float32,
    )
    slot_rank = jnp.sum(earlier * dest_onehot, axis=1).astype(jnp.int32)
    slot_onehot = (slot_rank[:, None] == jnp.arange(CAP, dtype=jnp.int32)[None, :]).astype(
        jnp.float32
    )
    selector = (dest_onehot[:, :, None] * slot_onehot[:, None, :]).reshape(rows, n_bands * CAP)

    index_lanes = jnp.broadcast_to(block_index[0].astype(jnp.float32)[:, None], (rows, 128))
    payload = jnp.concatenate([flux.reshape(rows, width), index_lanes], axis=1)
    sending = jnp.einsum("rk,rx->kx", selector, payload, precision=HIGHEST)
    sending = sending.reshape(n_bands, CAP, width + 128).astype(LINK)
    received = lax.all_to_all(sending, "band", 0, 0, tiled=True)
    received = received.reshape(n_bands * CAP, width + 128).astype(jnp.float32)
    got_index = received[:, width].astype(jnp.int32)
    match = (got_index[:, None] == positions[None, :]).astype(jnp.float32)
    partial = jnp.einsum("kr,kx->rx", match, received[:, :width], precision=HIGHEST)
    last = n_sections - 1
    scaled = (COUPLING * partial).astype(LINK)
    heating = scaled.astype(jnp.float32)
    for source in sorted(range(last), key=lambda t: (t + 1) % last):
        heating = heating + lax.ppermute(scaled, "comp", [(source, last)]).astype(jnp.float32)

    fields = diffuse(layer_temp, diffusivity)
    heating = jnp.where(is_ocean, heating, 0.0).reshape(rows, NF, cols)
    temp_out = fields.at[:, :NF].add(heating)
    returned = lax.cond(
        is_ocean,
        lambda: jnp.einsum(
            "rfc,rcd->rfd",
            (fields[:, :NF] + heating).astype(jnp.bfloat16),
            weights_local,
            preferred_element_type=jnp.float32,
        ).astype(jnp.bfloat16),
        lambda: jnp.zeros((rows, NF, cols), jnp.bfloat16),
    )

    spread = jnp.broadcast_to(returned[None], (n_sections, rows, NF, cols))
    ocean_rows = lax.all_to_all(spread, "comp", 0, 0, tiled=True)[last].reshape(rows, width)
    reply = jnp.einsum(
        "kr,rx->kx", match.astype(jnp.bfloat16), ocean_rows, preferred_element_type=jnp.float32
    ).astype(jnp.bfloat16)
    reply = reply.reshape(n_bands, CAP, width)
    came_back = lax.all_to_all(reply, "band", 0, 0, tiled=True)
    came_back = came_back.reshape(n_bands * CAP, width)
    seen = jnp.einsum(
        "rk,kx->rx", selector.astype(jnp.bfloat16), came_back, preferred_element_type=jnp.float32
    ).astype(jnp.bfloat16)
    surface_temp = jnp.where(is_ocean, returned, seen.reshape(rows, NF, cols))
    return temp_out[None], surface_temp[None]


def solution(mesh):
    return jax.shard_map(
        body,
        mesh=mesh,
        in_specs=(
            P("comp", "band", None, None),
            P("comp", "band", None),
            P("comp", "band", None),
            P("comp", "band"),
            P("comp", "band", None, None),
        ),
        out_specs=(P("comp", "band", None, None), P("comp", "band", None, None)),
        check_vma=False,
    )
```

```python
import jax
import jax.numpy as jnp
from jax import lax
from jax.sharding import PartitionSpec as P
from jax.experimental import pallas as pl
from jax.experimental.pallas import tpu as pltpu

NF = 4
NSTEPS = 4
CAP = 4

COUPLING = 0.25
VERTICAL = 0.15
HIGHEST = lax.Precision.HIGHEST
LINK = jnp.float16


def _advance_rows(src, dst, d_ref, r0, count, out_r0, bounds):
    lev, cols = dst.shape[1], dst.shape[2]
    fields = src[pl.ds(r0, count), pl.ds(0, lev)]
    row_north = src[pl.ds(r0 - 1, count), pl.ds(0, lev)]
    row_south = src[pl.ds(r0 + 1, count), pl.ds(0, lev)]
    diff = d_ref[pl.ds(r0, count), pl.ds(lev, 1)]
    level = lax.broadcasted_iota(jnp.int32, (count, lev, cols), 1)
    col_east = pltpu.roll(fields, 1, 2)
    col_west = pltpu.roll(fields, cols - 1, 2)
    level_below = jnp.where(level == 0, fields, pltpu.roll(fields, 1, 1))
    level_above = jnp.where(level == lev - 1, fields, pltpu.roll(fields, lev - 1, 1))
    horizontal = row_north + row_south + col_east + col_west - 4.0 * fields
    new = fields + diff * horizontal + VERTICAL * (level_below + level_above - 2.0 * fields)
    if bounds is not None:
        row = r0 + lax.broadcasted_iota(jnp.int32, (count, 1, 1), 0)
        new = jnp.where((row >= bounds[0]) & (row < bounds[1]), new, 0.0)
    dst[pl.ds(out_r0, count)] = new


def _largest_divisor(n, limit):
    return max(k for k in range(1, limit + 1) if n % k == 0)


def _diffusion_kernel(bounds_ref, p_ref, o_ref, buf_a, buf_b):
    total = p_ref.shape[0]
    rows, lev = o_ref.shape[0], o_ref.shape[1]
    halo = (total - rows) // 2
    bounds = (bounds_ref[0], bounds_ref[1])
    chunk = _largest_divisor(total - 2, 16)
    src = p_ref
    targets = (buf_a, buf_b)
    for step in range(NSTEPS - 1):
        dst = targets[step % 2]
        dst[0] = src[0, pl.ds(0, lev)]
        dst[total - 1] = src[total - 1, pl.ds(0, lev)]

        def one(i, carry, src=src, dst=dst):
            r0 = 1 + i * chunk
            _advance_rows(src, dst, p_ref, r0, chunk, r0, bounds)
            return carry

        lax.fori_loop(0, (total - 2) // chunk, one, 0)
        src = dst
    last = _largest_divisor(rows, 16)

    def final(i, carry):
        _advance_rows(src, o_ref, p_ref, halo + i * last, last, i * last, None)
        return carry

    lax.fori_loop(0, rows // last, final, 0)


def diffuse(layer_temp, diffusivity):
    n_bands = lax.axis_size("band")
    band = lax.axis_index("band")
    rows = layer_temp.shape[1]
    lev = layer_temp.shape[2]
    cols = layer_temp.shape[3]
    halo = NSTEPS
    total = rows + 2 * halo
    comb = jnp.concatenate([layer_temp[0], diffusivity[0][:, None, :]], axis=1)
    forward = [(i, i + 1) for i in range(n_bands - 1)]
    backward = [(i + 1, i) for i in range(n_bands - 1)]
    above = lax.ppermute(comb[rows - halo:], "band", forward)
    below = lax.ppermute(comb[:halo], "band", backward)
    padded = jnp.concatenate([above, comb, below], axis=0)
    first = jnp.where(band == 0, halo, 0)
    stop = jnp.where(band == n_bands - 1, halo + rows, total)
    bounds = jnp.stack([first, stop]).astype(jnp.int32)
    return pl.pallas_call(
        _diffusion_kernel,
        out_shape=jax.ShapeDtypeStruct((rows, lev, cols), jnp.float32),
        in_specs=[
            pl.BlockSpec(memory_space=pltpu.SMEM),
            pl.BlockSpec(memory_space=pltpu.VMEM),
        ],
        out_specs=pl.BlockSpec(memory_space=pltpu.VMEM),
        scratch_shapes=[pltpu.VMEM((total, lev, cols), jnp.float32)] * 2,
    )(bounds, padded)


def body(layer_temp, diffusivity, owner_band, block_index, remap_blocks):
    n_sections = lax.axis_size("comp")
    n_bands = lax.axis_size("band")
    section = lax.axis_index("comp")
    rows = layer_temp.shape[1]
    cols = layer_temp.shape[3]
    width = NF * cols
    is_ocean = section == n_sections - 1
    weights_local = remap_blocks[0]

    surface_layers = layer_temp[0, :, :NF, :].astype(jnp.bfloat16)
    flux = lax.cond(
        is_ocean,
        lambda: jnp.zeros((rows, NF, cols), jnp.float32),
        lambda: jnp.einsum(
            "rfc,rcd->rfd", surface_layers, weights_local, preferred_element_type=jnp.float32
        ),
    )

    destination = owner_band[0, :, 0]
    dest_onehot = (destination[:, None] == jnp.arange(n_bands, dtype=jnp.int32)[None, :]).astype(
        jnp.float32
    )
    positions = jnp.arange(rows, dtype=jnp.int32)
    same_earlier = (destination[:, None] == destination[None, :]) & (
        positions[:, None] > positions[None, :]
    )
    slot_rank = jnp.sum(same_earlier.astype(jnp.int32), axis=1)
    slot_onehot = (slot_rank[:, None] == jnp.arange(CAP, dtype=jnp.int32)[None, :]).astype(
        jnp.float32
    )
    selector = (dest_onehot[:, :, None] * slot_onehot[:, None, :]).reshape(rows, n_bands * CAP)

    index_lanes = jnp.broadcast_to(block_index[0].astype(jnp.float32)[:, None], (rows, 128))
    payload = jnp.concatenate([flux.reshape(rows, width), index_lanes], axis=1)
    sending = jnp.einsum("rk,rx->kx", selector, payload, precision=HIGHEST)
    sending = sending.reshape(n_bands, CAP, width + 128).astype(LINK)
    received = lax.all_to_all(sending, "band", 0, 0, tiled=True)
    received = received.reshape(n_bands * CAP, width + 128).astype(jnp.float32)
    got_index = received[:, width].astype(jnp.int32)
    match = (got_index[:, None] == positions[None, :]).astype(jnp.float32)
    partial = jnp.einsum("kr,kx->rx", match, received[:, :width], precision=HIGHEST)
    last = n_sections - 1
    scaled = (COUPLING * partial).astype(LINK)
    heating = scaled.astype(jnp.float32)
    for source in sorted(range(last), key=lambda t: (t + 1) % last):
        heating = heating + lax.ppermute(scaled, "comp", [(source, last)]).astype(jnp.float32)

    fields = diffuse(layer_temp, diffusivity)
    heating = jnp.where(is_ocean, heating, 0.0).reshape(rows, NF, cols)
    temp_out = fields.at[:, :NF].add(heating)
    returned = lax.cond(
        is_ocean,
        lambda: jnp.einsum(
            "rfc,rcd->rfd",
            (fields[:, :NF] + heating).astype(jnp.bfloat16),
            weights_local,
            preferred_element_type=jnp.float32,
        ).astype(jnp.bfloat16),
        lambda: jnp.zeros((rows, NF, cols), jnp.bfloat16),
    )

    ocean_rows = returned
    for target in sorted(range(last), key=lambda t: (t + 1) % last):
        ocean_rows = ocean_rows + lax.ppermute(returned, "comp", [(last, target)])
    ocean_rows = ocean_rows.reshape(rows, width)
    reply = jnp.einsum(
        "kr,rx->kx", match.astype(jnp.bfloat16), ocean_rows, preferred_element_type=jnp.float32
    ).astype(jnp.bfloat16)
    reply = reply.reshape(n_bands, CAP, width)
    came_back = lax.all_to_all(reply, "band", 0, 0, tiled=True)
    came_back = came_back.reshape(n_bands * CAP, width)
    seen = jnp.einsum(
        "rk,kx->rx", selector.astype(jnp.bfloat16), came_back, preferred_element_type=jnp.float32
    ).astype(jnp.bfloat16)
    surface_temp = jnp.where(is_ocean, returned, seen.reshape(rows, NF, cols))
    return temp_out[None], surface_temp[None]


def solution(mesh):
    return jax.shard_map(
        body,
        mesh=mesh,
        in_specs=(
            P("comp", "band", None, None),
            P("comp", "band", None),
            P("comp", "band", None),
            P("comp", "band"),
            P("comp", "band", None, None),
        ),
        out_specs=(P("comp", "band", None, None), P("comp", "band", None, None)),
        check_vma=False,
    )
```

```python
import jax
import jax.numpy as jnp
from jax import lax
from jax.sharding import PartitionSpec as P
from jax.experimental import pallas as pl
from jax.experimental.pallas import tpu as pltpu

NF = 4
NSTEPS = 4
CAP = 4

COUPLING = 0.25
VERTICAL = 0.15
HIGHEST = lax.Precision.HIGHEST
LINK = jnp.float16


def _advance_rows(src, dst, d_ref, r0, count, out_r0, bounds):
    lev, cols = dst.shape[1], dst.shape[2]
    fields = src[pl.ds(r0, count), pl.ds(0, lev)]
    row_north = src[pl.ds(r0 - 1, count), pl.ds(0, lev)]
    row_south = src[pl.ds(r0 + 1, count), pl.ds(0, lev)]
    diff = d_ref[pl.ds(r0, count), pl.ds(lev, 1)]
    level = lax.broadcasted_iota(jnp.int32, (count, lev, cols), 1)
    col_east = pltpu.roll(fields, 1, 2)
    col_west = pltpu.roll(fields, cols - 1, 2)
    level_below = jnp.where(level == 0, fields, pltpu.roll(fields, 1, 1))
    level_above = jnp.where(level == lev - 1, fields, pltpu.roll(fields, lev - 1, 1))
    horizontal = row_north + row_south + col_east + col_west - 4.0 * fields
    new = fields + diff * horizontal + VERTICAL * (level_below + level_above - 2.0 * fields)
    if bounds is not None:
        row = r0 + lax.broadcasted_iota(jnp.int32, (count, 1, 1), 0)
        new = jnp.where((row >= bounds[0]) & (row < bounds[1]), new, 0.0)
    dst[pl.ds(out_r0, count)] = new


def _largest_divisor(n, limit):
    return max(k for k in range(1, limit + 1) if n % k == 0)


def _diffusion_kernel(bounds_ref, p_ref, o_ref, buf_a, buf_b):
    total = p_ref.shape[0]
    rows, lev = o_ref.shape[0], o_ref.shape[1]
    halo = (total - rows) // 2
    bounds = (bounds_ref[0], bounds_ref[1])
    chunk = _largest_divisor(total - 2, 16)
    src = p_ref
    targets = (buf_a, buf_b)
    for step in range(NSTEPS - 1):
        dst = targets[step % 2]
        dst[0] = src[0, pl.ds(0, lev)]
        dst[total - 1] = src[total - 1, pl.ds(0, lev)]

        def one(i, carry, src=src, dst=dst):
            r0 = 1 + i * chunk
            _advance_rows(src, dst, p_ref, r0, chunk, r0, bounds)
            return carry

        lax.fori_loop(0, (total - 2) // chunk, one, 0)
        src = dst
    last = _largest_divisor(rows, 16)

    def final(i, carry):
        _advance_rows(src, o_ref, p_ref, halo + i * last, last, i * last, None)
        return carry

    lax.fori_loop(0, rows // last, final, 0)


def diffuse(layer_temp, diffusivity):
    n_bands = lax.axis_size("band")
    band = lax.axis_index("band")
    rows = layer_temp.shape[1]
    lev = layer_temp.shape[2]
    cols = layer_temp.shape[3]
    halo = NSTEPS
    total = rows + 2 * halo
    comb = jnp.concatenate([layer_temp[0], diffusivity[0][:, None, :]], axis=1)
    forward = [(i, i + 1) for i in range(n_bands - 1)]
    backward = [(i + 1, i) for i in range(n_bands - 1)]
    above = lax.ppermute(comb[rows - halo:], "band", forward)
    below = lax.ppermute(comb[:halo], "band", backward)
    padded = jnp.concatenate([above, comb, below], axis=0)
    first = jnp.where(band == 0, halo, 0)
    stop = jnp.where(band == n_bands - 1, halo + rows, total)
    bounds = jnp.stack([first, stop]).astype(jnp.int32)
    return pl.pallas_call(
        _diffusion_kernel,
        out_shape=jax.ShapeDtypeStruct((rows, lev, cols), jnp.float32),
        in_specs=[
            pl.BlockSpec(memory_space=pltpu.SMEM),
            pl.BlockSpec(memory_space=pltpu.VMEM),
        ],
        out_specs=pl.BlockSpec(memory_space=pltpu.VMEM),
        scratch_shapes=[pltpu.VMEM((total, lev, cols), jnp.float32)] * 2,
    )(bounds, padded)


def body(layer_temp, diffusivity, owner_band, block_index, remap_blocks):
    n_sections = lax.axis_size("comp")
    n_bands = lax.axis_size("band")
    section = lax.axis_index("comp")
    rows = layer_temp.shape[1]
    cols = layer_temp.shape[3]
    width = NF * cols
    is_ocean = section == n_sections - 1
    weights_local = remap_blocks[0]

    surface_layers = layer_temp[0, :, :NF, :].astype(jnp.bfloat16)
    flux = lax.cond(
        is_ocean,
        lambda: jnp.zeros((rows, NF, cols), jnp.float32),
        lambda: jnp.einsum(
            "rfc,rcd->rfd", surface_layers, weights_local, preferred_element_type=jnp.float32
        ),
    )

    destination = owner_band[0, :, 0]
    dest_onehot = (destination[:, None] == jnp.arange(n_bands, dtype=jnp.int32)[None, :]).astype(
        jnp.float32
    )
    positions = jnp.arange(rows, dtype=jnp.int32)
    earlier_mask = (positions[:, None] > positions[None, :]).astype(jnp.float32)
    earlier = jnp.dot(
        earlier_mask.astype(jnp.bfloat16),
        dest_onehot.astype(jnp.bfloat16),
        preferred_element_type=jnp.float32,
    )
    slot_rank = jnp.sum(earlier * dest_onehot, axis=1).astype(jnp.int32)
    slot_onehot = (slot_rank[:, None] == jnp.arange(CAP, dtype=jnp.int32)[None, :]).astype(
        jnp.float32
    )
    selector = (dest_onehot[:, :, None] * slot_onehot[:, None, :]).reshape(rows, n_bands * CAP)

    index_lanes = jnp.broadcast_to(block_index[0].astype(jnp.float32)[:, None], (rows, 128))
    payload = jnp.concatenate([flux.reshape(rows, width), index_lanes], axis=1)
    sending = jnp.einsum("rk,rx->kx", selector, payload, precision=HIGHEST)
    sending = sending.reshape(n_bands, CAP, width + 128).astype(LINK)
    received = lax.all_to_all(sending, "band", 0, 0, tiled=True)
    received = received.reshape(n_bands * CAP, width + 128).astype(jnp.float32)
    got_index = received[:, width].astype(jnp.int32)
    match = (got_index[:, None] == positions[None, :]).astype(jnp.float32)
    partial = jnp.einsum("kr,kx->rx", match, received[:, :width], precision=HIGHEST)
    last = n_sections - 1
    scaled = (COUPLING * partial).astype(LINK)
    heating = scaled.astype(jnp.float32)
    for source in sorted(range(last), key=lambda t: (t + 1) % last):
        heating = heating + lax.ppermute(scaled, "comp", [(source, last)]).astype(jnp.float32)

    fields = diffuse(layer_temp, diffusivity)
    heating = jnp.where(is_ocean, heating, 0.0).reshape(rows, NF, cols)
    temp_out = fields.at[:, :NF].add(heating)
    returned = lax.cond(
        is_ocean,
        lambda: jnp.einsum(
            "rfc,rcd->rfd",
            (fields[:, :NF] + heating).astype(jnp.bfloat16),
            weights_local,
            preferred_element_type=jnp.float32,
        ).astype(jnp.bfloat16),
        lambda: jnp.zeros((rows, NF, cols), jnp.bfloat16),
    )

    ocean_rows = returned
    for target in sorted(range(last), reverse=True):
        ocean_rows = ocean_rows + lax.ppermute(returned, "comp", [(last, target)])
    ocean_rows = ocean_rows.reshape(rows, width)
    reply = jnp.einsum(
        "kr,rx->kx", match.astype(jnp.bfloat16), ocean_rows, preferred_element_type=jnp.float32
    ).astype(jnp.bfloat16)
    reply = reply.reshape(n_bands, CAP, width)
    came_back = lax.all_to_all(reply, "band", 0, 0, tiled=True)
    came_back = came_back.reshape(n_bands * CAP, width)
    seen = jnp.einsum(
        "rk,kx->rx", selector.astype(jnp.bfloat16), came_back, preferred_element_type=jnp.float32
    ).astype(jnp.bfloat16)
    surface_temp = jnp.where(is_ocean, returned, seen.reshape(rows, NF, cols))
    return temp_out[None], surface_temp[None]


def solution(mesh):
    return jax.shard_map(
        body,
        mesh=mesh,
        in_specs=(
            P("comp", "band", None, None),
            P("comp", "band", None),
            P("comp", "band", None),
            P("comp", "band"),
            P("comp", "band", None, None),
        ),
        out_specs=(P("comp", "band", None, None), P("comp", "band", None, None)),
        check_vma=False,
    )
```

```python
import jax
import jax.numpy as jnp
from jax import lax
from jax.sharding import PartitionSpec as P
from jax.experimental import pallas as pl
from jax.experimental.pallas import tpu as pltpu

NF = 4
NSTEPS = 4
CAP = 4

COUPLING = 0.25
VERTICAL = 0.15
HIGHEST = lax.Precision.HIGHEST
LINK = jnp.float16


def _advance_rows(src, dst, d_ref, r0, count, out_r0, bounds):
    lev, cols = dst.shape[1], dst.shape[2]
    fields = src[pl.ds(r0, count), pl.ds(0, lev)]
    row_north = src[pl.ds(r0 - 1, count), pl.ds(0, lev)]
    row_south = src[pl.ds(r0 + 1, count), pl.ds(0, lev)]
    diff = d_ref[pl.ds(r0, count), pl.ds(lev, 1)]
    level = lax.broadcasted_iota(jnp.int32, (count, lev, cols), 1)
    col_east = pltpu.roll(fields, 1, 2)
    col_west = pltpu.roll(fields, cols - 1, 2)
    level_below = jnp.where(level == 0, fields, pltpu.roll(fields, 1, 1))
    level_above = jnp.where(level == lev - 1, fields, pltpu.roll(fields, lev - 1, 1))
    horizontal = row_north + row_south + col_east + col_west - 4.0 * fields
    new = fields + diff * horizontal + VERTICAL * (level_below + level_above - 2.0 * fields)
    if bounds is not None:
        row = r0 + lax.broadcasted_iota(jnp.int32, (count, 1, 1), 0)
        new = jnp.where((row >= bounds[0]) & (row < bounds[1]), new, 0.0)
    dst[pl.ds(out_r0, count)] = new


def _largest_divisor(n, limit):
    return max(k for k in range(1, limit + 1) if n % k == 0)


def _diffusion_kernel(bounds_ref, p_ref, o_ref, buf_a, buf_b):
    total = p_ref.shape[0]
    rows, lev = o_ref.shape[0], o_ref.shape[1]
    halo = (total - rows) // 2
    bounds = (bounds_ref[0], bounds_ref[1])
    chunk = _largest_divisor(total - 2, 16)
    src = p_ref
    targets = (buf_a, buf_b)
    for step in range(NSTEPS - 1):
        dst = targets[step % 2]
        dst[0] = src[0, pl.ds(0, lev)]
        dst[total - 1] = src[total - 1, pl.ds(0, lev)]

        def one(i, carry, src=src, dst=dst):
            r0 = 1 + i * chunk
            _advance_rows(src, dst, p_ref, r0, chunk, r0, bounds)
            return carry

        lax.fori_loop(0, (total - 2) // chunk, one, 0)
        src = dst
    last = _largest_divisor(rows, 16)

    def final(i, carry):
        _advance_rows(src, o_ref, p_ref, halo + i * last, last, i * last, None)
        return carry

    lax.fori_loop(0, rows // last, final, 0)


def diffuse(layer_temp, diffusivity):
    n_bands = lax.axis_size("band")
    band = lax.axis_index("band")
    rows = layer_temp.shape[1]
    lev = layer_temp.shape[2]
    cols = layer_temp.shape[3]
    halo = NSTEPS
    total = rows + 2 * halo
    comb = jnp.concatenate([layer_temp[0], diffusivity[0][:, None, :]], axis=1)
    forward = [(i, i + 1) for i in range(n_bands - 1)]
    backward = [(i + 1, i) for i in range(n_bands - 1)]
    above = lax.ppermute(comb[rows - halo:], "band", forward)
    below = lax.ppermute(comb[:halo], "band", backward)
    padded = jnp.concatenate([above, comb, below], axis=0)
    first = jnp.where(band == 0, halo, 0)
    stop = jnp.where(band == n_bands - 1, halo + rows, total)
    bounds = jnp.stack([first, stop]).astype(jnp.int32)
    return pl.pallas_call(
        _diffusion_kernel,
        out_shape=jax.ShapeDtypeStruct((rows, lev, cols), jnp.float32),
        in_specs=[
            pl.BlockSpec(memory_space=pltpu.SMEM),
            pl.BlockSpec(memory_space=pltpu.VMEM),
        ],
        out_specs=pl.BlockSpec(memory_space=pltpu.VMEM),
        scratch_shapes=[pltpu.VMEM((total, lev, cols), jnp.float32)] * 2,
    )(bounds, padded)


def body(layer_temp, diffusivity, owner_band, block_index, remap_blocks):
    n_sections = lax.axis_size("comp")
    n_bands = lax.axis_size("band")
    section = lax.axis_index("comp")
    rows = layer_temp.shape[1]
    cols = layer_temp.shape[3]
    width = NF * cols
    is_ocean = section == n_sections - 1
    weights_local = remap_blocks[0]

    surface_layers = layer_temp[0, :, :NF, :].astype(jnp.bfloat16)
    flux = lax.cond(
        is_ocean,
        lambda: jnp.zeros((rows, NF, cols), jnp.float32),
        lambda: jnp.einsum(
            "rfc,rcd->rfd", surface_layers, weights_local, preferred_element_type=jnp.float32
        ),
    )

    destination = owner_band[0, :, 0]
    dest_onehot = (destination[:, None] == jnp.arange(n_bands, dtype=jnp.int32)[None, :]).astype(
        jnp.float32
    )
    positions = jnp.arange(rows, dtype=jnp.int32)
    earlier_mask = (positions[:, None] > positions[None, :]).astype(jnp.float32)
    earlier = jnp.dot(
        earlier_mask.astype(jnp.bfloat16),
        dest_onehot.astype(jnp.bfloat16),
        preferred_element_type=jnp.float32,
    )
    slot_rank = jnp.sum(earlier * dest_onehot, axis=1).astype(jnp.int32)
    slot_onehot = (slot_rank[:, None] == jnp.arange(CAP, dtype=jnp.int32)[None, :]).astype(
        jnp.float32
    )
    selector = (dest_onehot[:, :, None] * slot_onehot[:, None, :]).reshape(rows, n_bands * CAP)

    index_lanes = jnp.broadcast_to(block_index[0].astype(jnp.float32)[:, None], (rows, 128))
    payload = jnp.concatenate([flux.reshape(rows, width), index_lanes], axis=1)
    sending = jnp.einsum("rk,rx->kx", selector, payload, precision=HIGHEST)
    sending = sending.reshape(n_bands, CAP, width + 128).astype(LINK)
    received = lax.all_to_all(sending, "band", 0, 0, tiled=True)
    received = received.reshape(n_bands * CAP, width + 128).astype(jnp.float32)
    got_index = received[:, width].astype(jnp.int32)
    match = (got_index[:, None] == positions[None, :]).astype(jnp.float32)
    partial = jnp.einsum("kr,kx->rx", match, received[:, :width], precision=HIGHEST)
    last = n_sections - 1
    scaled = (COUPLING * partial).astype(LINK)
    heating = scaled.astype(jnp.float32)
    for source in sorted(range(last), reverse=True):
        heating = heating + lax.ppermute(scaled, "comp", [(source, last)]).astype(jnp.float32)

    fields = diffuse(layer_temp, diffusivity)
    heating = jnp.where(is_ocean, heating, 0.0).reshape(rows, NF, cols)
    temp_out = fields.at[:, :NF].add(heating)
    returned = lax.cond(
        is_ocean,
        lambda: jnp.einsum(
            "rfc,rcd->rfd",
            (fields[:, :NF] + heating).astype(jnp.bfloat16),
            weights_local,
            preferred_element_type=jnp.float32,
        ).astype(jnp.bfloat16),
        lambda: jnp.zeros((rows, NF, cols), jnp.bfloat16),
    )

    ocean_rows = returned
    for target in sorted(range(last), reverse=True):
        ocean_rows = ocean_rows + lax.ppermute(returned, "comp", [(last, target)])
    ocean_rows = ocean_rows.reshape(rows, width)
    reply = jnp.einsum(
        "kr,rx->kx", match.astype(jnp.bfloat16), ocean_rows, preferred_element_type=jnp.float32
    ).astype(jnp.bfloat16)
    reply = reply.reshape(n_bands, CAP, width)
    came_back = lax.all_to_all(reply, "band", 0, 0, tiled=True)
    came_back = came_back.reshape(n_bands * CAP, width)
    seen = jnp.einsum(
        "rk,kx->rx", selector.astype(jnp.bfloat16), came_back, preferred_element_type=jnp.float32
    ).astype(jnp.bfloat16)
    surface_temp = jnp.where(is_ocean, returned, seen.reshape(rows, NF, cols))
    return temp_out[None], surface_temp[None]


def solution(mesh):
    return jax.shard_map(
        body,
        mesh=mesh,
        in_specs=(
            P("comp", "band", None, None),
            P("comp", "band", None),
            P("comp", "band", None),
            P("comp", "band"),
            P("comp", "band", None, None),
        ),
        out_specs=(P("comp", "band", None, None), P("comp", "band", None, None)),
        check_vma=False,
    )
```

```python
import jax
import jax.numpy as jnp
from jax import lax
from jax.sharding import PartitionSpec as P
from jax.experimental import pallas as pl
from jax.experimental.pallas import tpu as pltpu

NF = 4
NSTEPS = 4
CAP = 4

COUPLING = 0.25
VERTICAL = 0.15
HIGHEST = lax.Precision.HIGHEST
LINK = jnp.float16


def _advance_rows(src, dst, d_ref, r0, count, out_r0, bounds):
    lev, cols = dst.shape[1], dst.shape[2]
    fields = src[pl.ds(r0, count), pl.ds(0, lev)]
    row_north = src[pl.ds(r0 - 1, count), pl.ds(0, lev)]
    row_south = src[pl.ds(r0 + 1, count), pl.ds(0, lev)]
    diff = d_ref[pl.ds(r0, count), pl.ds(lev, 1)]
    level = lax.broadcasted_iota(jnp.int32, (count, lev, cols), 1)
    col_east = pltpu.roll(fields, 1, 2)
    col_west = pltpu.roll(fields, cols - 1, 2)
    level_below = jnp.where(level == 0, fields, pltpu.roll(fields, 1, 1))
    level_above = jnp.where(level == lev - 1, fields, pltpu.roll(fields, lev - 1, 1))
    horizontal = row_north + row_south + col_east + col_west - 4.0 * fields
    new = fields + diff * horizontal + VERTICAL * (level_below + level_above - 2.0 * fields)
    if bounds is not None:
        row = r0 + lax.broadcasted_iota(jnp.int32, (count, 1, 1), 0)
        new = jnp.where((row >= bounds[0]) & (row < bounds[1]), new, 0.0)
    dst[pl.ds(out_r0, count)] = new


def _largest_divisor(n, limit):
    return max(k for k in range(1, limit + 1) if n % k == 0)


def _diffusion_kernel(bounds_ref, above_ref, comb_ref, below_ref, o_ref, p_ref, buf_a, buf_b):
    total = p_ref.shape[0]
    halo_rows = above_ref.shape[0]
    p_ref[pl.ds(0, halo_rows)] = above_ref[...]
    p_ref[pl.ds(halo_rows, comb_ref.shape[0])] = comb_ref[...]
    p_ref[pl.ds(total - halo_rows, halo_rows)] = below_ref[...]
    rows, lev = o_ref.shape[0], o_ref.shape[1]
    halo = (total - rows) // 2
    bounds = (bounds_ref[0], bounds_ref[1])
    chunk = _largest_divisor(total - 2, 16)
    src = p_ref
    targets = (buf_a, buf_b)
    for step in range(NSTEPS - 1):
        dst = targets[step % 2]
        dst[0] = src[0, pl.ds(0, lev)]
        dst[total - 1] = src[total - 1, pl.ds(0, lev)]

        def one(i, carry, src=src, dst=dst):
            r0 = 1 + i * chunk
            _advance_rows(src, dst, p_ref, r0, chunk, r0, bounds)
            return carry

        lax.fori_loop(0, (total - 2) // chunk, one, 0)
        src = dst
    last = _largest_divisor(rows, 16)

    def final(i, carry):
        _advance_rows(src, o_ref, p_ref, halo + i * last, last, i * last, None)
        return carry

    lax.fori_loop(0, rows // last, final, 0)


def diffuse(layer_temp, diffusivity):
    n_bands = lax.axis_size("band")
    band = lax.axis_index("band")
    rows = layer_temp.shape[1]
    lev = layer_temp.shape[2]
    cols = layer_temp.shape[3]
    halo = NSTEPS
    total = rows + 2 * halo
    comb = jnp.concatenate([layer_temp[0], diffusivity[0][:, None, :]], axis=1)
    forward = [(i, i + 1) for i in range(n_bands - 1)]
    backward = [(i + 1, i) for i in range(n_bands - 1)]
    above = lax.ppermute(comb[rows - halo:], "band", forward)
    below = lax.ppermute(comb[:halo], "band", backward)
    first = jnp.where(band == 0, halo, 0)
    stop = jnp.where(band == n_bands - 1, halo + rows, total)
    bounds = jnp.stack([first, stop]).astype(jnp.int32)
    return pl.pallas_call(
        _diffusion_kernel,
        out_shape=jax.ShapeDtypeStruct((rows, lev, cols), jnp.float32),
        in_specs=[
            pl.BlockSpec(memory_space=pltpu.SMEM),
            pl.BlockSpec(memory_space=pltpu.VMEM),
            pl.BlockSpec(memory_space=pltpu.VMEM),
            pl.BlockSpec(memory_space=pltpu.VMEM),
        ],
        out_specs=pl.BlockSpec(memory_space=pltpu.VMEM),
        scratch_shapes=[pltpu.VMEM((total, lev + 1, cols), jnp.float32)]
        + [pltpu.VMEM((total, lev, cols), jnp.float32)] * 2,
    )(bounds, above, comb, below)


def body(layer_temp, diffusivity, owner_band, block_index, remap_blocks):
    n_sections = lax.axis_size("comp")
    n_bands = lax.axis_size("band")
    section = lax.axis_index("comp")
    rows = layer_temp.shape[1]
    cols = layer_temp.shape[3]
    width = NF * cols
    is_ocean = section == n_sections - 1
    weights_local = remap_blocks[0]

    surface_layers = layer_temp[0, :, :NF, :].astype(jnp.bfloat16)
    flux = lax.cond(
        is_ocean,
        lambda: jnp.zeros((rows, NF, cols), jnp.float32),
        lambda: jnp.einsum(
            "rfc,rcd->rfd", surface_layers, weights_local, preferred_element_type=jnp.float32
        ),
    )

    destination = owner_band[0, :, 0]
    dest_onehot = (destination[:, None] == jnp.arange(n_bands, dtype=jnp.int32)[None, :]).astype(
        jnp.float32
    )
    positions = jnp.arange(rows, dtype=jnp.int32)
    earlier_mask = (positions[:, None] > positions[None, :]).astype(jnp.float32)
    earlier = jnp.dot(
        earlier_mask.astype(jnp.bfloat16),
        dest_onehot.astype(jnp.bfloat16),
        preferred_element_type=jnp.float32,
    )
    slot_rank = jnp.sum(earlier * dest_onehot, axis=1).astype(jnp.int32)
    slot_onehot = (slot_rank[:, None] == jnp.arange(CAP, dtype=jnp.int32)[None, :]).astype(
        jnp.float32
    )
    selector = (dest_onehot[:, :, None] * slot_onehot[:, None, :]).reshape(rows, n_bands * CAP)

    index_lanes = jnp.broadcast_to(block_index[0].astype(jnp.float32)[:, None], (rows, 128))
    payload = jnp.concatenate([flux.reshape(rows, width), index_lanes], axis=1)
    sending = jnp.einsum("rk,rx->kx", selector, payload, precision=HIGHEST)
    sending = sending.reshape(n_bands, CAP, width + 128).astype(LINK)
    received = lax.all_to_all(sending, "band", 0, 0, tiled=True)
    received = received.reshape(n_bands * CAP, width + 128).astype(jnp.float32)
    got_index = received[:, width].astype(jnp.int32)
    match = (got_index[:, None] == positions[None, :]).astype(jnp.float32)
    partial = jnp.einsum("kr,kx->rx", match, received[:, :width], precision=HIGHEST)
    last = n_sections - 1
    scaled = (COUPLING * partial).astype(LINK)
    heating = scaled.astype(jnp.float32)
    for source in sorted(range(last), reverse=True):
        heating = heating + lax.ppermute(scaled, "comp", [(source, last)]).astype(jnp.float32)

    fields = diffuse(layer_temp, diffusivity)
    heating = jnp.where(is_ocean, heating, 0.0).reshape(rows, NF, cols)
    temp_out = fields.at[:, :NF].add(heating)
    returned = lax.cond(
        is_ocean,
        lambda: jnp.einsum(
            "rfc,rcd->rfd",
            (fields[:, :NF] + heating).astype(jnp.bfloat16),
            weights_local,
            preferred_element_type=jnp.float32,
        ).astype(jnp.bfloat16),
        lambda: jnp.zeros((rows, NF, cols), jnp.bfloat16),
    )

    ocean_rows = returned
    for target in sorted(range(last), reverse=True):
        ocean_rows = ocean_rows + lax.ppermute(returned, "comp", [(last, target)])
    ocean_rows = ocean_rows.reshape(rows, width)
    reply = jnp.einsum(
        "kr,rx->kx", match.astype(jnp.bfloat16), ocean_rows, preferred_element_type=jnp.float32
    ).astype(jnp.bfloat16)
    reply = reply.reshape(n_bands, CAP, width)
    came_back = lax.all_to_all(reply, "band", 0, 0, tiled=True)
    came_back = came_back.reshape(n_bands * CAP, width)
    seen = jnp.einsum(
        "rk,kx->rx", selector.astype(jnp.bfloat16), came_back, preferred_element_type=jnp.float32
    ).astype(jnp.bfloat16)
    surface_temp = jnp.where(is_ocean, returned, seen.reshape(rows, NF, cols))
    return temp_out[None], surface_temp[None]


def solution(mesh):
    return jax.shard_map(
        body,
        mesh=mesh,
        in_specs=(
            P("comp", "band", None, None),
            P("comp", "band", None),
            P("comp", "band", None),
            P("comp", "band"),
            P("comp", "band", None, None),
        ),
        out_specs=(P("comp", "band", None, None), P("comp", "band", None, None)),
        check_vma=False,
    )
```

```python
import jax
import jax.numpy as jnp
from jax import lax
from jax.sharding import PartitionSpec as P
from jax.experimental import pallas as pl
from jax.experimental.pallas import tpu as pltpu

NF = 4
NSTEPS = 4
CAP = 4

COUPLING = 0.25
VERTICAL = 0.15
HIGHEST = lax.Precision.HIGHEST
LINK = jnp.float16


def _advance_rows(src, dst, d_ref, r0, count, out_r0, bounds):
    lev, cols = dst.shape[1], dst.shape[2]
    fields = src[pl.ds(r0, count), pl.ds(0, lev)]
    row_north = src[pl.ds(r0 - 1, count), pl.ds(0, lev)]
    row_south = src[pl.ds(r0 + 1, count), pl.ds(0, lev)]
    diff = d_ref[pl.ds(r0, count), pl.ds(lev, 1)]
    level = lax.broadcasted_iota(jnp.int32, (count, lev, cols), 1)
    col_east = pltpu.roll(fields, 1, 2)
    col_west = pltpu.roll(fields, cols - 1, 2)
    level_below = jnp.where(level == 0, fields, pltpu.roll(fields, 1, 1))
    level_above = jnp.where(level == lev - 1, fields, pltpu.roll(fields, lev - 1, 1))
    horizontal = row_north + row_south + col_east + col_west - 4.0 * fields
    new = fields + diff * horizontal + VERTICAL * (level_below + level_above - 2.0 * fields)
    if bounds is not None:
        row = r0 + lax.broadcasted_iota(jnp.int32, (count, 1, 1), 0)
        new = jnp.where((row >= bounds[0]) & (row < bounds[1]), new, 0.0)
    dst[pl.ds(out_r0, count)] = new


def _largest_divisor(n, limit):
    return max(k for k in range(1, limit + 1) if n % k == 0)


def _diffusion_kernel(bounds_ref, p_ref, o_ref, buf_a, buf_b):
    total = p_ref.shape[0]
    rows, lev = o_ref.shape[0], o_ref.shape[1]
    halo = (total - rows) // 2
    bounds = (bounds_ref[0], bounds_ref[1])
    chunk = _largest_divisor(total - 2, 16)
    src = p_ref
    targets = (buf_a, buf_b)
    for step in range(NSTEPS - 1):
        dst = targets[step % 2]
        dst[0] = src[0, pl.ds(0, lev)]
        dst[total - 1] = src[total - 1, pl.ds(0, lev)]

        def one(i, carry, src=src, dst=dst):
            r0 = 1 + i * chunk
            _advance_rows(src, dst, p_ref, r0, chunk, r0, bounds)
            return carry

        lax.fori_loop(0, (total - 2) // chunk, one, 0)
        src = dst
    last = _largest_divisor(rows, 16)

    def final(i, carry):
        _advance_rows(src, o_ref, p_ref, halo + i * last, last, i * last, None)
        return carry

    lax.fori_loop(0, rows // last, final, 0)


def diffuse(layer_temp, diffusivity):
    n_bands = lax.axis_size("band")
    band = lax.axis_index("band")
    rows = layer_temp.shape[1]
    lev = layer_temp.shape[2]
    cols = layer_temp.shape[3]
    halo = NSTEPS
    total = rows + 2 * halo
    comb = jnp.concatenate([layer_temp[0], diffusivity[0][:, None, :]], axis=1)
    forward = [(i, i + 1) for i in range(n_bands - 1)]
    backward = [(i + 1, i) for i in range(n_bands - 1)]
    above = lax.ppermute(comb[rows - halo:], "band", forward)
    below = lax.ppermute(comb[:halo], "band", backward)
    padded = jnp.concatenate([above, comb, below], axis=0)
    first = jnp.where(band == 0, halo, 0)
    stop = jnp.where(band == n_bands - 1, halo + rows, total)
    bounds = jnp.stack([first, stop]).astype(jnp.int32)
    return pl.pallas_call(
        _diffusion_kernel,
        out_shape=jax.ShapeDtypeStruct((rows, lev, cols), jnp.float32),
        in_specs=[
            pl.BlockSpec(memory_space=pltpu.SMEM),
            pl.BlockSpec(memory_space=pltpu.VMEM),
        ],
        out_specs=pl.BlockSpec(memory_space=pltpu.VMEM),
        scratch_shapes=[pltpu.VMEM((total, lev, cols), jnp.float32)] * 2,
    )(bounds, padded)


def body(layer_temp, diffusivity, owner_band, block_index, remap_blocks):
    n_sections = lax.axis_size("comp")
    n_bands = lax.axis_size("band")
    section = lax.axis_index("comp")
    rows = layer_temp.shape[1]
    cols = layer_temp.shape[3]
    width = NF * cols
    is_ocean = section == n_sections - 1
    weights_local = remap_blocks[0]

    surface_layers = layer_temp[0, :, :NF, :].astype(jnp.bfloat16)
    flux = lax.cond(
        is_ocean,
        lambda: jnp.zeros((rows, NF, cols), jnp.float32),
        lambda: jnp.einsum(
            "rfc,rcd->rfd", surface_layers, weights_local, preferred_element_type=jnp.float32
        ),
    )

    destination = owner_band[0, :, 0]
    dest_onehot = (destination[:, None] == jnp.arange(n_bands, dtype=jnp.int32)[None, :]).astype(
        jnp.float32
    )
    positions = jnp.arange(rows, dtype=jnp.int32)
    earlier_mask = (positions[:, None] > positions[None, :]).astype(jnp.float32)
    earlier = jnp.dot(
        earlier_mask.astype(jnp.bfloat16),
        dest_onehot.astype(jnp.bfloat16),
        preferred_element_type=jnp.float32,
    )
    slot_rank = jnp.sum(earlier * dest_onehot, axis=1).astype(jnp.int32)
    slot_onehot = (slot_rank[:, None] == jnp.arange(CAP, dtype=jnp.int32)[None, :]).astype(
        jnp.float32
    )
    selector = (dest_onehot[:, :, None] * slot_onehot[:, None, :]).reshape(rows, n_bands * CAP)

    index_lanes = jnp.broadcast_to(block_index[0].astype(jnp.float32)[:, None], (rows, 128))
    payload = jnp.concatenate([flux.reshape(rows, width), index_lanes], axis=1)
    sending = jnp.einsum("rk,rx->kx", selector, payload, precision=HIGHEST)
    sending = sending.reshape(n_bands, CAP, width + 128).astype(LINK)
    received = lax.all_to_all(sending, "band", 0, 0, tiled=True)
    received = received.reshape(n_bands * CAP, width + 128).astype(jnp.float32)
    got_index = received[:, width].astype(jnp.int32)
    match = (got_index[:, None] == positions[None, :]).astype(jnp.float32)
    partial = jnp.einsum("kr,kx->rx", match, received[:, :width], precision=HIGHEST)
    last = n_sections - 1
    scaled = (COUPLING * partial).astype(LINK)
    heating = scaled.astype(jnp.float32)
    for source in sorted(range(last), reverse=True):
        heating = heating + lax.ppermute(scaled, "comp", [(source, last)]).astype(jnp.float32)

    fields = diffuse(layer_temp, diffusivity)
    heating = jnp.where(is_ocean, heating, 0.0).reshape(rows, NF, cols)
    temp_out = fields.at[:, :NF].add(heating)
    returned = lax.cond(
        is_ocean,
        lambda: jnp.einsum(
            "rfc,rcd->rfd",
            (fields[:, :NF] + heating).astype(jnp.bfloat16),
            weights_local,
            preferred_element_type=jnp.float32,
        ).astype(jnp.bfloat16),
        lambda: jnp.zeros((rows, NF, cols), jnp.bfloat16),
    )

    ocean_rows = returned
    for target in sorted(range(last), key=lambda t: (t + 1) % last):
        ocean_rows = ocean_rows + lax.ppermute(returned, "comp", [(last, target)])
    ocean_rows = ocean_rows.reshape(rows, width)
    reply = jnp.einsum(
        "kr,rx->kx", match.astype(jnp.bfloat16), ocean_rows, preferred_element_type=jnp.float32
    ).astype(jnp.bfloat16)
    reply = reply.reshape(n_bands, CAP, width)
    came_back = lax.all_to_all(reply, "band", 0, 0, tiled=True)
    came_back = came_back.reshape(n_bands * CAP, width)
    seen = jnp.einsum(
        "rk,kx->rx", selector.astype(jnp.bfloat16), came_back, preferred_element_type=jnp.float32
    ).astype(jnp.bfloat16)
    surface_temp = jnp.where(is_ocean, returned, seen.reshape(rows, NF, cols))
    return temp_out[None], surface_temp[None]


def solution(mesh):
    return jax.shard_map(
        body,
        mesh=mesh,
        in_specs=(
            P("comp", "band", None, None),
            P("comp", "band", None),
            P("comp", "band", None),
            P("comp", "band"),
            P("comp", "band", None, None),
        ),
        out_specs=(P("comp", "band", None, None), P("comp", "band", None, None)),
        check_vma=False,
    )
```

```python
import jax
import jax.numpy as jnp
from jax import lax
from jax.sharding import PartitionSpec as P
from jax.experimental import pallas as pl
from jax.experimental.pallas import tpu as pltpu

NF = 4
NSTEPS = 4
CAP = 4

COUPLING = 0.25
VERTICAL = 0.15
HIGHEST = lax.Precision.HIGHEST
LINK = jnp.float16


def _advance_rows(src, dst, d_ref, r0, count, out_r0, bounds):
    lev, cols = dst.shape[1], dst.shape[2]
    fields = src[pl.ds(r0, count), pl.ds(0, lev)]
    row_north = src[pl.ds(r0 - 1, count), pl.ds(0, lev)]
    row_south = src[pl.ds(r0 + 1, count), pl.ds(0, lev)]
    diff = d_ref[pl.ds(r0, count), pl.ds(lev, 1)]
    level = lax.broadcasted_iota(jnp.int32, (count, lev, cols), 1)
    col_east = pltpu.roll(fields, 1, 2)
    col_west = pltpu.roll(fields, cols - 1, 2)
    level_below = jnp.where(level == 0, fields, pltpu.roll(fields, 1, 1))
    level_above = jnp.where(level == lev - 1, fields, pltpu.roll(fields, lev - 1, 1))
    horizontal = row_north + row_south + col_east + col_west - 4.0 * fields
    new = fields + diff * horizontal + VERTICAL * (level_below + level_above - 2.0 * fields)
    if bounds is not None:
        row = r0 + lax.broadcasted_iota(jnp.int32, (count, 1, 1), 0)
        new = jnp.where((row >= bounds[0]) & (row < bounds[1]), new, 0.0)
    dst[pl.ds(out_r0, count)] = new


def _largest_divisor(n, limit):
    return max(k for k in range(1, limit + 1) if n % k == 0)


def _diffusion_kernel(bounds_ref, p_ref, o_ref, buf_a, buf_b):
    total = p_ref.shape[0]
    rows, lev = o_ref.shape[0], o_ref.shape[1]
    halo = (total - rows) // 2
    bounds = (bounds_ref[0], bounds_ref[1])
    chunk = _largest_divisor(total - 2, 16)
    src = p_ref
    targets = (buf_a, buf_b)
    for step in range(NSTEPS - 1):
        dst = targets[step % 2]
        dst[0] = src[0, pl.ds(0, lev)]
        dst[total - 1] = src[total - 1, pl.ds(0, lev)]

        def one(i, carry, src=src, dst=dst):
            r0 = 1 + i * chunk
            _advance_rows(src, dst, p_ref, r0, chunk, r0, bounds)
            return carry

        lax.fori_loop(0, (total - 2) // chunk, one, 0)
        src = dst
    last = _largest_divisor(rows, 16)

    def final(i, carry):
        _advance_rows(src, o_ref, p_ref, halo + i * last, last, i * last, None)
        return carry

    lax.fori_loop(0, rows // last, final, 0)


def diffuse(layer_temp, diffusivity):
    n_bands = lax.axis_size("band")
    band = lax.axis_index("band")
    rows = layer_temp.shape[1]
    lev = layer_temp.shape[2]
    cols = layer_temp.shape[3]
    halo = NSTEPS
    total = rows + 2 * halo
    comb = jnp.concatenate([layer_temp[0], diffusivity[0][:, None, :]], axis=1)
    forward = [(i, i + 1) for i in range(n_bands - 1)]
    backward = [(i + 1, i) for i in range(n_bands - 1)]
    above = lax.ppermute(comb[rows - halo:], "band", forward)
    below = lax.ppermute(comb[:halo], "band", backward)
    padded = jnp.concatenate([above, comb, below], axis=0)
    first = jnp.where(band == 0, halo, 0)
    stop = jnp.where(band == n_bands - 1, halo + rows, total)
    bounds = jnp.stack([first, stop]).astype(jnp.int32)
    return pl.pallas_call(
        _diffusion_kernel,
        out_shape=jax.ShapeDtypeStruct((rows, lev, cols), jnp.float32),
        in_specs=[
            pl.BlockSpec(memory_space=pltpu.SMEM),
            pl.BlockSpec(memory_space=pltpu.VMEM),
        ],
        out_specs=pl.BlockSpec(memory_space=pltpu.VMEM),
        scratch_shapes=[pltpu.VMEM((total, lev, cols), jnp.float32)] * 2,
    )(bounds, padded)


def body(layer_temp, diffusivity, owner_band, block_index, remap_blocks):
    n_sections = lax.axis_size("comp")
    n_bands = lax.axis_size("band")
    section = lax.axis_index("comp")
    rows = layer_temp.shape[1]
    cols = layer_temp.shape[3]
    width = NF * cols
    is_ocean = section == n_sections - 1
    weights_local = remap_blocks[0]

    surface_layers = layer_temp[0, :, :NF, :].astype(jnp.bfloat16)
    flux = lax.cond(
        is_ocean,
        lambda: jnp.zeros((rows, NF, cols), jnp.float32),
        lambda: jnp.einsum(
            "rfc,rcd->rfd", surface_layers, weights_local, preferred_element_type=jnp.float32
        ),
    )

    destination = owner_band[0, :, 0]
    dest_onehot = (destination[:, None] == jnp.arange(n_bands, dtype=jnp.int32)[None, :]).astype(
        jnp.float32
    )
    positions = jnp.arange(rows, dtype=jnp.int32)
    earlier_mask = (positions[:, None] > positions[None, :]).astype(jnp.float32)
    earlier = jnp.dot(
        earlier_mask.astype(jnp.bfloat16),
        dest_onehot.astype(jnp.bfloat16),
        preferred_element_type=jnp.float32,
    )
    slot_rank = jnp.sum(earlier * dest_onehot, axis=1).astype(jnp.int32)
    slot_onehot = (slot_rank[:, None] == jnp.arange(CAP, dtype=jnp.int32)[None, :]).astype(
        jnp.float32
    )
    selector = (dest_onehot[:, :, None] * slot_onehot[:, None, :]).reshape(rows, n_bands * CAP)

    index_lanes = jnp.broadcast_to(block_index[0].astype(jnp.float32)[:, None], (rows, 128))
    payload = jnp.concatenate([flux.reshape(rows, width), index_lanes], axis=1)
    sending = jnp.einsum("rk,rx->kx", selector, payload, precision=HIGHEST)
    sending = sending.reshape(n_bands, CAP, width + 128).astype(LINK)
    received = lax.all_to_all(sending, "band", 0, 0, tiled=True)
    received = received.reshape(n_bands * CAP, width + 128).astype(jnp.float32)
    got_index = received[:, width].astype(jnp.int32)
    match = (got_index[:, None] == positions[None, :]).astype(jnp.float32)
    partial = jnp.einsum("kr,kx->rx", match, received[:, :width], precision=HIGHEST)
    last = n_sections - 1
    scaled = (COUPLING * partial).astype(LINK)
    heating = scaled.astype(jnp.float32)
    for source in sorted(range(last), reverse=True):
        heating = heating + lax.ppermute(scaled, "comp", [(source, last)]).astype(jnp.float32)

    fields = diffuse(layer_temp, diffusivity)
    heating = jnp.where(is_ocean, heating, 0.0).reshape(rows, NF, cols)
    temp_out = fields.at[:, :NF].add(heating)
    returned = lax.cond(
        is_ocean,
        lambda: jnp.einsum(
            "rfc,rcd->rfd",
            (fields[:, :NF] + heating).astype(jnp.bfloat16),
            weights_local,
            preferred_element_type=jnp.float32,
        ).astype(jnp.bfloat16),
        lambda: jnp.zeros((rows, NF, cols), jnp.bfloat16),
    )

    ocean_rows = returned
    for target in (1, 2, 0):
        ocean_rows = ocean_rows + lax.ppermute(returned, "comp", [(last, target)])
    ocean_rows = ocean_rows.reshape(rows, width)
    reply = jnp.einsum(
        "kr,rx->kx", match.astype(jnp.bfloat16), ocean_rows, preferred_element_type=jnp.float32
    ).astype(jnp.bfloat16)
    reply = reply.reshape(n_bands, CAP, width)
    came_back = lax.all_to_all(reply, "band", 0, 0, tiled=True)
    came_back = came_back.reshape(n_bands * CAP, width)
    seen = jnp.einsum(
        "rk,kx->rx", selector.astype(jnp.bfloat16), came_back, preferred_element_type=jnp.float32
    ).astype(jnp.bfloat16)
    surface_temp = jnp.where(is_ocean, returned, seen.reshape(rows, NF, cols))
    return temp_out[None], surface_temp[None]


def solution(mesh):
    return jax.shard_map(
        body,
        mesh=mesh,
        in_specs=(
            P("comp", "band", None, None),
            P("comp", "band", None),
            P("comp", "band", None),
            P("comp", "band"),
            P("comp", "band", None, None),
        ),
        out_specs=(P("comp", "band", None, None), P("comp", "band", None, None)),
        check_vma=False,
    )
```

```python
import jax
import jax.numpy as jnp
from jax import lax
from jax.sharding import PartitionSpec as P
from jax.experimental import pallas as pl
from jax.experimental.pallas import tpu as pltpu

NF = 4
NSTEPS = 4
CAP = 4

COUPLING = 0.25
VERTICAL = 0.15
HIGHEST = lax.Precision.HIGHEST
LINK = jnp.float16


def _advance_rows(src, dst, d_ref, r0, count, out_r0, bounds):
    lev, cols = dst.shape[1], dst.shape[2]
    fields = src[pl.ds(r0, count), pl.ds(0, lev)]
    row_north = src[pl.ds(r0 - 1, count), pl.ds(0, lev)]
    row_south = src[pl.ds(r0 + 1, count), pl.ds(0, lev)]
    diff = d_ref[pl.ds(r0, count), pl.ds(lev, 1)]
    level = lax.broadcasted_iota(jnp.int32, (count, lev, cols), 1)
    col_east = pltpu.roll(fields, 1, 2)
    col_west = pltpu.roll(fields, cols - 1, 2)
    level_below = jnp.where(level == 0, fields, pltpu.roll(fields, 1, 1))
    level_above = jnp.where(level == lev - 1, fields, pltpu.roll(fields, lev - 1, 1))
    horizontal = row_north + row_south + col_east + col_west - 4.0 * fields
    new = fields + diff * horizontal + VERTICAL * (level_below + level_above - 2.0 * fields)
    if bounds is not None:
        row = r0 + lax.broadcasted_iota(jnp.int32, (count, 1, 1), 0)
        new = jnp.where((row >= bounds[0]) & (row < bounds[1]), new, 0.0)
    dst[pl.ds(out_r0, count)] = new


def _largest_divisor(n, limit):
    return max(k for k in range(1, limit + 1) if n % k == 0)


def _diffusion_kernel(bounds_ref, p_ref, o_ref, buf_a, buf_b):
    total = p_ref.shape[0]
    rows, lev = o_ref.shape[0], o_ref.shape[1]
    halo = (total - rows) // 2
    bounds = (bounds_ref[0], bounds_ref[1])
    chunk = _largest_divisor(total - 2, 16)
    src = p_ref
    targets = (buf_a, buf_b)
    for step in range(NSTEPS - 1):
        dst = targets[step % 2]
        dst[0] = src[0, pl.ds(0, lev)]
        dst[total - 1] = src[total - 1, pl.ds(0, lev)]

        def one(i, carry, src=src, dst=dst):
            r0 = 1 + i * chunk
            _advance_rows(src, dst, p_ref, r0, chunk, r0, bounds)
            return carry

        lax.fori_loop(0, (total - 2) // chunk, one, 0)
        src = dst
    last = _largest_divisor(rows, 16)

    def final(i, carry):
        _advance_rows(src, o_ref, p_ref, halo + i * last, last, i * last, None)
        return carry

    lax.fori_loop(0, rows // last, final, 0)


def diffuse(layer_temp, diffusivity):
    n_bands = lax.axis_size("band")
    band = lax.axis_index("band")
    rows = layer_temp.shape[1]
    lev = layer_temp.shape[2]
    cols = layer_temp.shape[3]
    halo = NSTEPS
    total = rows + 2 * halo
    comb = jnp.concatenate([layer_temp[0], diffusivity[0][:, None, :]], axis=1)
    forward = [(i, i + 1) for i in range(n_bands - 1)]
    backward = [(i + 1, i) for i in range(n_bands - 1)]
    above = lax.ppermute(comb[rows - halo:], "band", forward)
    below = lax.ppermute(comb[:halo], "band", backward)
    padded = jnp.concatenate([above, comb, below], axis=0)
    first = jnp.where(band == 0, halo, 0)
    stop = jnp.where(band == n_bands - 1, halo + rows, total)
    bounds = jnp.stack([first, stop]).astype(jnp.int32)
    return pl.pallas_call(
        _diffusion_kernel,
        out_shape=jax.ShapeDtypeStruct((rows, lev, cols), jnp.float32),
        in_specs=[
            pl.BlockSpec(memory_space=pltpu.SMEM),
            pl.BlockSpec(memory_space=pltpu.VMEM),
        ],
        out_specs=pl.BlockSpec(memory_space=pltpu.VMEM),
        scratch_shapes=[pltpu.VMEM((total, lev, cols), jnp.float32)] * 2,
    )(bounds, padded)


def body(layer_temp, diffusivity, owner_band, block_index, remap_blocks):
    n_sections = lax.axis_size("comp")
    n_bands = lax.axis_size("band")
    section = lax.axis_index("comp")
    rows = layer_temp.shape[1]
    cols = layer_temp.shape[3]
    width = NF * cols
    is_ocean = section == n_sections - 1
    weights_local = remap_blocks[0]

    surface_layers = layer_temp[0, :, :NF, :].astype(jnp.bfloat16)
    flux = lax.cond(
        is_ocean,
        lambda: jnp.zeros((rows, NF, cols), jnp.float32),
        lambda: jnp.einsum(
            "rfc,rcd->rfd", surface_layers, weights_local, preferred_element_type=jnp.float32
        ),
    )

    destination = owner_band[0, :, 0]
    dest_onehot = (destination[:, None] == jnp.arange(n_bands, dtype=jnp.int32)[None, :]).astype(
        jnp.float32
    )
    positions = jnp.arange(rows, dtype=jnp.int32)
    earlier_mask = (positions[:, None] > positions[None, :]).astype(jnp.float32)
    earlier = jnp.dot(
        earlier_mask.astype(jnp.bfloat16),
        dest_onehot.astype(jnp.bfloat16),
        preferred_element_type=jnp.float32,
    )
    slot_rank = jnp.sum(earlier * dest_onehot, axis=1).astype(jnp.int32)
    slot_onehot = (slot_rank[:, None] == jnp.arange(CAP, dtype=jnp.int32)[None, :]).astype(
        jnp.float32
    )
    selector = (dest_onehot[:, :, None] * slot_onehot[:, None, :]).reshape(rows, n_bands * CAP)

    index_lanes = jnp.broadcast_to(block_index[0].astype(jnp.float32)[:, None], (rows, 128))
    payload = jnp.concatenate([flux.reshape(rows, width), index_lanes], axis=1)
    sending = jnp.einsum("rk,rx->kx", selector, payload, precision=HIGHEST)
    sending = sending.reshape(n_bands, CAP, width + 128).astype(LINK)
    received = lax.all_to_all(sending, "band", 0, 0, tiled=True)
    received = received.reshape(n_bands * CAP, width + 128).astype(jnp.float32)
    got_index = received[:, width].astype(jnp.int32)
    match = (got_index[:, None] == positions[None, :]).astype(jnp.float32)
    partial = jnp.einsum("kr,kx->rx", match, received[:, :width], precision=HIGHEST)
    last = n_sections - 1
    scaled = (COUPLING * partial).astype(LINK)
    heating = scaled.astype(jnp.float32)
    for source in (1, 2, 0):
        heating = heating + lax.ppermute(scaled, "comp", [(source, last)]).astype(jnp.float32)

    fields = diffuse(layer_temp, diffusivity)
    heating = jnp.where(is_ocean, heating, 0.0).reshape(rows, NF, cols)
    temp_out = fields.at[:, :NF].add(heating)
    returned = lax.cond(
        is_ocean,
        lambda: jnp.einsum(
            "rfc,rcd->rfd",
            (fields[:, :NF] + heating).astype(jnp.bfloat16),
            weights_local,
            preferred_element_type=jnp.float32,
        ).astype(jnp.bfloat16),
        lambda: jnp.zeros((rows, NF, cols), jnp.bfloat16),
    )

    ocean_rows = returned
    for target in sorted(range(last), reverse=True):
        ocean_rows = ocean_rows + lax.ppermute(returned, "comp", [(last, target)])
    ocean_rows = ocean_rows.reshape(rows, width)
    reply = jnp.einsum(
        "kr,rx->kx", match.astype(jnp.bfloat16), ocean_rows, preferred_element_type=jnp.float32
    ).astype(jnp.bfloat16)
    reply = reply.reshape(n_bands, CAP, width)
    came_back = lax.all_to_all(reply, "band", 0, 0, tiled=True)
    came_back = came_back.reshape(n_bands * CAP, width)
    seen = jnp.einsum(
        "rk,kx->rx", selector.astype(jnp.bfloat16), came_back, preferred_element_type=jnp.float32
    ).astype(jnp.bfloat16)
    surface_temp = jnp.where(is_ocean, returned, seen.reshape(rows, NF, cols))
    return temp_out[None], surface_temp[None]


def solution(mesh):
    return jax.shard_map(
        body,
        mesh=mesh,
        in_specs=(
            P("comp", "band", None, None),
            P("comp", "band", None),
            P("comp", "band", None),
            P("comp", "band"),
            P("comp", "band", None, None),
        ),
        out_specs=(P("comp", "band", None, None), P("comp", "band", None, None)),
        check_vma=False,
    )
```
